128 devices in a mesh: ctx: 32 (over y, z, core), tp: 4 (over x).
Axes of the slice: x: 4, y: 4, z: 4, core: 2. Of those that a mesh axis runs over, the one named last changes fastest.
Arguments:
- hidden_in: bfloat16 [16384, 4608], P('ctx'), may hold values from -5.4 to 5.4
- pre_gain: float32 [4608], replicated, may hold values from 0.25 to 1.75
- w_query: bfloat16 [4608, 2048], P(None, 'tp'), may hold values from -0.677644 to 0.677644
- w_key: bfloat16 [4608, 1024], P(None, 'tp'), may hold values from -0.058925565 to 0.058925565
- w_value: bfloat16 [4608, 1024], P(None, 'tp'), may hold values from -0.09375 to 0.09375
- w_out: bfloat16 [2048, 4608], P('tp'), may hold values from -0.26516504 to 0.26516504
- post_gain: float32 [4608], P('tp'), may hold values from 0.25 to 1.75
Outputs:
- layer_out: bfloat16 [16384, 4608], P('ctx', 'tp')
- sink_share: float32 [16384], P('ctx')
The draws below stay inside these ranges and needn't reach their ends.
All inputs are finite; a program needn't handle non-finite values.
Results may differ from the reference program's by a relative error of at most 0.0095.
The reference program's roundings to bfloat16 on the way (of `normed`, `weight16` and `attended`) count: a program that leaves them out, or rounds other values in their place, can miss the bound.
Values may be sent and summed in bfloat16 or wider, within the bound.
No kernel may reach another device: no remote copies, remote signals or barrier semaphores. Data moves between devices by JAX's collectives and lax.ppermute only.
A program may use at most 192 MiB of HBM per device.

```python
import jax
import jax.numpy as jnp
from jax import lax

D = 4608
QHEADS = 16
KVHEADS = 8
HEAD = 128
WINDOW = 4096
SINKS = 4
TOKENS = 16384


def draw_hidden_in(key, part):
    first, second, third = jax.random.split(key, 3)
    row_scale = jnp.exp(jax.random.uniform(second, (TOKENS, 1), jnp.float32, jnp.log(jnp.float32(0.03)), jnp.log(jnp.float32(0.3))))
    col_scale = jnp.exp(jax.random.uniform(third, (1, D), jnp.float32, jnp.log(jnp.float32(0.3)), jnp.log(jnp.float32(3.0))))
    base = jnp.clip(jax.random.normal(first, (TOKENS, D), jnp.float32), -6.0, 6.0)
    return (base * row_scale * col_scale).astype(jnp.bfloat16)


def key_columns(key):
    base = jax.random.normal(jax.random.fold_in(key, 101), (D, KVHEADS * HEAD), jnp.float32)
    return jnp.clip(base, -4.0, 4.0) * float(D) ** (-0.5)


def draw_w_key(key, part):
    return key_columns(key).astype(jnp.bfloat16)


def draw_w_query(key, part):
    half = HEAD // 2
    columns = key_columns(key).reshape(D, KVHEADS, HEAD)
    index = jnp.arange(half).astype(jnp.float32) * 2.0
    inverse = jnp.exp(-jnp.log(jnp.float32(10000.0)) * index / HEAD)
    phase = jnp.float32(WINDOW // 2) * inverse
    cosine = jnp.cos(phase)
    sine = jnp.sin(phase)
    first_half = columns[..., :half]
    second_half = columns[..., half:]
    turned = 8.0 * jnp.concatenate([first_half * cosine + second_half * sine, second_half * cosine - first_half * sine], axis=-1)
    turned = jnp.repeat(turned, QHEADS // KVHEADS, axis=1)
    drawn = jnp.clip(jax.random.normal(jax.random.fold_in(key, 102), (D, QHEADS, HEAD), jnp.float32), -4.0, 4.0) * float(D) ** (-0.5)
    order = jax.random.permutation(jax.random.fold_in(key, 103), QHEADS)
    chosen = (order < QHEADS // 4)[None, :, None]
    return jnp.where(chosen, turned, drawn).reshape(D, QHEADS * HEAD).astype(jnp.bfloat16)


def draw_w_out(key, part):
    first = jax.random.fold_in(key, 201)
    second = jax.random.fold_in(key, 202)
    fan_rows = QHEADS * HEAD
    col_scale = jnp.exp(jax.random.uniform(second, (1, D), jnp.float32, jnp.log(jnp.float32(0.3)), jnp.log(jnp.float32(3.0))))
    base = jnp.clip(jax.random.normal(first, (fan_rows, D), jnp.float32), -4.0, 4.0)
    return (base * col_scale * float(fan_rows) ** (-0.5)).astype(jnp.bfloat16)


def block_scale(rng, dims, pieces, least, largest):
    gain, own = 1.0, jax.random.fold_in(rng, 6)
    for axis_at, shards_of in pieces:
        draws = jnp.exp(jax.random.uniform(jax.random.fold_in(own, axis_at), (shards_of,), jnp.float32, least / len(pieces), largest / len(pieces)))
        gain = gain * jnp.repeat(draws, dims[axis_at] // shards_of).reshape([-1 if axis == axis_at else 1 for axis in range(len(dims))])
    return gain


def gaussian(stream_key, shape, spread, most, cuts=(), kind=jnp.bfloat16):
    drawn = jax.random.normal(stream_key, shape, jnp.float32) * spread
    if len(cuts) > 0:
        drawn = block_scale(stream_key, shape, cuts, -0.22, 0.18) * drawn
    return jnp.clip(drawn, min=-most, max=most).astype(kind)


def setup_inputs(seed: int = 0) -> dict:
    streams_of = jax.random.split(jax.random.key(seed), 8)
    hidden_in = draw_hidden_in(jax.random.fold_in(streams_of[7], 71), 0)
    pre_gain = jnp.clip(1.0 + 0.15 * jax.random.normal(streams_of[1], (D,), jnp.float32), 0.25, 1.75)
    w_query = draw_w_query(jax.random.fold_in(streams_of[7], 71), 0)
    w_key = draw_w_key(jax.random.fold_in(streams_of[7], 71), 0)
    w_value = gaussian(streams_of[4], (D, KVHEADS * HEAD), D ** -0.5, 0.09375, ((1, 4),))
    w_out = draw_w_out(jax.random.fold_in(streams_of[7], 71), 0)
    post_gain = jnp.clip(1.0 + 0.15 * jax.random.normal(streams_of[6], (D,), jnp.float32), 0.25, 1.75)
    return {"hidden_in": hidden_in, "pre_gain": pre_gain, "w_query": w_query, "w_key": w_key, "w_value": w_value, "w_out": w_out, "post_gain": post_gain}


def rope_tables(positions):
    index = jnp.arange(0, HEAD, 2).astype(jnp.float32)
    inverse = jnp.exp(-jnp.log(jnp.float32(10000.0)) * index / HEAD)
    angles = positions.astype(jnp.float32)[:, None] * inverse[None, :]
    angles = jnp.concatenate([angles, angles], axis=1)
    return (jnp.cos(angles)[:, None, :], jnp.sin(angles)[:, None, :])

def rotate(values, cosine_table, sine_table):
    half = values.shape[-1] // 2
    turned = jnp.concatenate([-values[..., half:], values[..., :half]], axis=-1)
    return values * cosine_table + turned * sine_table

def reference(hidden_in, pre_gain, w_query, w_key, w_value, w_out, post_gain):
    inputs = hidden_in.astype(jnp.float32)
    normed = (inputs * lax.rsqrt(lax.optimization_barrier(jnp.mean(inputs * inputs, axis=-1, keepdims=True)) + 1e-06) * pre_gain).astype(jnp.bfloat16)
    cosine_table, sine_table = rope_tables(jnp.arange(TOKENS))
    query = jnp.dot(normed, w_query, preferred_element_type=jnp.float32).reshape(TOKENS, QHEADS, HEAD)
    query = rotate(query, cosine_table, sine_table).astype(jnp.bfloat16)
    keys = jnp.dot(normed, w_key, preferred_element_type=jnp.float32).reshape(TOKENS, KVHEADS, HEAD)
    keys = rotate(keys, cosine_table, sine_table).astype(jnp.bfloat16)
    values = jnp.dot(normed, w_value, preferred_element_type=jnp.float32).reshape(TOKENS, KVHEADS, HEAD).astype(jnp.bfloat16)
    padding = jnp.zeros((WINDOW, KVHEADS, HEAD), jnp.bfloat16)
    keys_padded = jnp.concatenate([padding, keys], axis=0)
    values_padded = jnp.concatenate([padding, values], axis=0)
    sink_keys = keys[:SINKS].astype(jnp.float32)
    sink_values = values[:SINKS].astype(jnp.float32)
    group = QHEADS // KVHEADS
    block_rows = min(512, TOKENS)
    span = WINDOW + block_rows

    def one_block(block_index):
        start = (block_index * block_rows).astype(jnp.int32)
        query_block = lax.dynamic_slice_in_dim(query, start, block_rows, 0).astype(jnp.float32).reshape(block_rows, KVHEADS, group, HEAD)
        key_block = lax.dynamic_slice_in_dim(keys_padded, start, span, 0).astype(jnp.float32)
        value_block = lax.dynamic_slice_in_dim(values_padded, start, span, 0).astype(jnp.float32)
        scores = jnp.einsum('qkgd,lkd->kgql', query_block, key_block) / 12.0
        scores = 50.0 * jnp.tanh(scores / 50.0)
        sink_scores = jnp.einsum('qkgd,lkd->kgql', query_block, sink_keys) / 12.0
        sink_scores = 50.0 * jnp.tanh(sink_scores / 50.0)
        query_pos = start + jnp.arange(block_rows, dtype=jnp.int32)
        key_pos = start - WINDOW + jnp.arange(span, dtype=jnp.int32)
        distance = query_pos[:, None] - key_pos[None, :]
        live = (key_pos[None, :] >= SINKS) & (distance >= 0) & (distance < WINDOW)
        sink_live = query_pos[:, None] - jnp.arange(SINKS, dtype=jnp.int32)[None, :] >= 0
        expo = jnp.where(live, jnp.exp(scores), 0.0)
        sink_expo = jnp.where(sink_live, jnp.exp(sink_scores), 0.0)
        total = lax.optimization_barrier(jnp.sum(expo, axis=-1)) + lax.optimization_barrier(jnp.sum(sink_expo, axis=-1))
        weight = expo / total[..., None]
        sink_weight = sink_expo / total[..., None]
        sink_sum = lax.optimization_barrier(jnp.sum(sink_expo, axis=-1))
        weight16 = weight.astype(jnp.bfloat16).astype(jnp.float32)
        sink16 = sink_weight.astype(jnp.bfloat16).astype(jnp.float32)
        attended = jnp.einsum('kgql,lkd->qkgd', weight16, value_block) + jnp.einsum('kgql,lkd->qkgd', sink16, sink_values)
        attended = attended.astype(jnp.bfloat16).reshape(block_rows, QHEADS * HEAD)
        return (attended, lax.optimization_barrier(jnp.sum(sink_sum, axis=(0, 1))))
    attended, sink_sums = lax.map(one_block, jnp.arange(TOKENS // block_rows, dtype=jnp.int32))
    attended = attended.reshape(TOKENS, QHEADS * HEAD)
    sink_sums = sink_sums.reshape(TOKENS)
    projected = jnp.dot(attended, w_out, preferred_element_type=jnp.float32)
    post = projected * lax.rsqrt(lax.optimization_barrier(jnp.mean(projected * projected, axis=-1, keepdims=True)) + 1e-06) * post_gain
    layer_out = (inputs + post).astype(jnp.bfloat16)
    sink_share = jnp.log(sink_sums / QHEADS)
    return (layer_out, sink_share)
```

```python
import jax
import jax.numpy as jnp
from jax import lax
from jax.sharding import PartitionSpec as P

D = 4608
QHEADS = 16
HEAD = 128
WINDOW = 4096
SINKS = 4


def shifted(x, axis, by):
    devices = lax.axis_size(axis)
    pairs = [(i, i + by) for i in range(devices) if 0 <= i + by < devices]
    return lax.ppermute(x, axis, pairs)


def cyclic(x, axis, by):
    devices = lax.axis_size(axis)
    return lax.ppermute(x, axis, [(i, (i + by) % devices) for i in range(devices)])


def rope_tables(positions):
    index = jnp.arange(0, HEAD, 2).astype(jnp.float32)
    inverse = jnp.exp(-jnp.log(jnp.float32(10000.0)) * index / HEAD)
    angles = positions.astype(jnp.float32)[:, None] * inverse[None, :]
    angles = jnp.concatenate([angles, angles], axis=1)
    return (jnp.cos(angles)[:, None, :], jnp.sin(angles)[:, None, :])


def rotate(values, cosine_table, sine_table):
    half = values.shape[-1] // 2
    turned = jnp.concatenate([-values[..., half:], values[..., :half]], axis=-1)
    return values * cosine_table + turned * sine_table


def on_device(hidden_in, pre_gain, w_query, w_key, w_value, w_out, post_gain):
    tok_rows = hidden_in.shape[0]
    local_q = w_query.shape[1] // HEAD
    local_kv = w_key.shape[1] // HEAD
    group = local_q // local_kv
    kv_cols = local_kv * HEAD
    tp_n = lax.axis_size("tp")
    tp_i = lax.axis_index("tp")
    cols_dev = post_gain.shape[0]

    w_blocks = w_out.reshape(w_out.shape[0], tp_n, cols_dev)
    w_recv = []
    for k in range(tp_n):
        part = lax.dynamic_index_in_dim(w_blocks, (tp_i + k) % tp_n, axis=1, keepdims=False)
        w_recv.append(part if k == 0 else cyclic(part, "tp", k))

    offset = lax.axis_index("ctx") * tok_rows
    inputs = hidden_in.astype(jnp.float32)
    normed = (
        inputs * lax.rsqrt(jnp.mean(inputs * inputs, axis=-1, keepdims=True) + 1e-06) * pre_gain
    ).astype(jnp.bfloat16)
    positions = offset + jnp.arange(tok_rows, dtype=jnp.int32)
    cosine_table, sine_table = rope_tables(positions)
    query = jnp.dot(normed, w_query, preferred_element_type=jnp.float32).reshape(
        tok_rows, local_q, HEAD
    )
    query = (
        rotate(query, cosine_table, sine_table)
        .astype(jnp.bfloat16)
        .reshape(tok_rows, local_kv, group, HEAD)
    )
    keys = jnp.dot(normed, w_key, preferred_element_type=jnp.float32).reshape(tok_rows, -1, HEAD)
    keys = rotate(keys, cosine_table, sine_table).astype(jnp.bfloat16).reshape(tok_rows, -1)
    values = jnp.dot(normed, w_value, preferred_element_type=jnp.float32).astype(jnp.bfloat16)
    kv = jnp.concatenate([keys, values], axis=1)

    sink_kv = lax.all_gather(kv[:SINKS], "ctx")[0]
    reach = WINDOW // tok_rows
    pieces = [shifted(kv, "ctx", distance) for distance in range(reach, 0, -1)]
    kv_all = jnp.concatenate(pieces + [kv], axis=0)
    span = WINDOW + tok_rows
    key_block = kv_all[:, :kv_cols].reshape(span, local_kv, HEAD)
    value_block = kv_all[:, kv_cols:].reshape(span, local_kv, HEAD)
    sink_keys = sink_kv[:, :kv_cols].reshape(SINKS, local_kv, HEAD)
    sink_values = sink_kv[:, kv_cols:].reshape(SINKS, local_kv, HEAD)

    scores = (
        jnp.einsum("qkgd,lkd->kgql", query, key_block, preferred_element_type=jnp.float32) / 12.0
    )
    scores = 50.0 * jnp.tanh(scores / 50.0)
    sink_scores = (
        jnp.einsum("qkgd,lkd->kgql", query, sink_keys, preferred_element_type=jnp.float32) / 12.0
    )
    sink_scores = 50.0 * jnp.tanh(sink_scores / 50.0)
    query_pos = positions
    key_pos = offset - WINDOW + jnp.arange(span, dtype=jnp.int32)
    distance_map = query_pos[:, None] - key_pos[None, :]
    live = (key_pos[None, :] >= SINKS) & (distance_map >= 0) & (distance_map < WINDOW)
    sink_live = query_pos[:, None] - jnp.arange(SINKS, dtype=jnp.int32)[None, :] >= 0
    expo = jnp.where(live, jnp.exp(scores), 0.0)
    sink_expo = jnp.where(sink_live, jnp.exp(sink_scores), 0.0)
    sink_sum = jnp.sum(sink_expo, axis=-1)
    total = jnp.sum(expo, axis=-1) + sink_sum
    weight = expo / total[..., None]
    sink_weight = sink_expo / total[..., None]
    attended = jnp.einsum(
        "kgql,lkd->qkgd", weight.astype(jnp.bfloat16), value_block,
        preferred_element_type=jnp.float32,
    )
    attended = attended + jnp.einsum(
        "kgql,lkd->qkgd", sink_weight.astype(jnp.bfloat16), sink_values,
        preferred_element_type=jnp.float32,
    )
    attended = attended.astype(jnp.bfloat16).reshape(tok_rows, local_q * HEAD)
    sink_sums = jnp.sum(sink_sum, axis=(0, 1))

    projected = jnp.dot(attended, w_recv[0], preferred_element_type=jnp.float32)
    for k in range(1, tp_n):
        projected = projected + jnp.dot(
            cyclic(attended, "tp", k), w_recv[k], preferred_element_type=jnp.float32
        )
    squares = jnp.sum(projected * projected, axis=-1)
    total_squares, total_sinks = lax.psum((squares, sink_sums), "tp")
    post = projected * lax.rsqrt(total_squares / D + 1e-06)[:, None] * post_gain
    own_cols = lax.dynamic_slice_in_dim(inputs, tp_i * cols_dev, cols_dev, 1)
    layer_out = (own_cols + post).astype(jnp.bfloat16)
    sink_share = jnp.log(total_sinks / QHEADS)
    return (layer_out, sink_share)


def solution(mesh):
    return jax.shard_map(
        on_device,
        mesh=mesh,
        in_specs=(
            P("ctx", None),
            P(),
            P(None, "tp"),
            P(None, "tp"),
            P(None, "tp"),
            P("tp", None),
            P("tp"),
        ),
        out_specs=(P("ctx", "tp"), P("ctx")),
        check_vma=False,
    )
```

```python
import jax
import jax.numpy as jnp
from jax import lax
from jax.experimental import pallas as pl
from jax.experimental.pallas import tpu as pltpu
from jax.sharding import PartitionSpec as P

D = 4608
QHEADS = 16
HEAD = 128
WINDOW = 4096
SINKS = 4


def shifted(x, axis, by):
    devices = lax.axis_size(axis)
    pairs = [(i, i + by) for i in range(devices) if 0 <= i + by < devices]
    return lax.ppermute(x, axis, pairs)


def cyclic(x, axis, by):
    devices = lax.axis_size(axis)
    return lax.ppermute(x, axis, [(i, (i + by) % devices) for i in range(devices)])


def rope_tables(positions):
    index = jnp.arange(0, HEAD, 2).astype(jnp.float32)
    inverse = jnp.exp(-jnp.log(jnp.float32(10000.0)) * index / HEAD)
    angles = positions.astype(jnp.float32)[:, None] * inverse[None, :]
    angles = jnp.concatenate([angles, angles], axis=1)
    return (jnp.cos(angles)[:, None, :], jnp.sin(angles)[:, None, :])


def rotate(values, cosine_table, sine_table):
    half = values.shape[-1] // 2
    turned = jnp.concatenate([-values[..., half:], values[..., :half]], axis=-1)
    return values * cosine_table + turned * sine_table


def window_attention(query2d, kv_all, sink_kv, offset, local_kv, group, tq=256, chunk=256):
    tok_rows = query2d.shape[0]
    span = kv_all.shape[0]
    rows = group * tq
    win = WINDOW + tq
    nchunks = win // chunk
    n_qt = tok_rows // tq

    def kernel(off_ref, q_ref, k_ref, v_ref, sk_ref, sv_ref, o_ref, ss_ref, expo_scr, acc_scr, rs_scr):
        i = pl.program_id(1)
        q0 = i * tq
        base = off_ref[0] - WINDOW + q0
        qb = q_ref[...]
        q = jnp.concatenate([qb[:, g * HEAD:(g + 1) * HEAD] for g in range(group)], axis=0)
        qi = lax.broadcasted_iota(jnp.int32, (rows, 1), 0) % tq
        lo = jnp.maximum(qi + 1, SINKS - base)
        hi = qi + WINDOW
        rs_scr[...] = jnp.zeros((rows, 128), jnp.float32)

        def pass1(c, carry):
            start = pl.multiple_of(q0 + c * chunk, chunk)
            kc = k_ref[pl.ds(start, chunk), :]
            s = lax.dot_general(q, kc, (((1,), (1,)), ((), ())), preferred_element_type=jnp.float32)
            t = 50.0 * jnp.tanh(s * (1.0 / 600.0))
            col = c * chunk + lax.broadcasted_iota(jnp.int32, (1, chunk), 1)
            live = (col >= lo) & (col <= hi)
            e = jnp.where(live, jnp.exp(t), 0.0)
            expo_scr[c] = e
            part = e[:, 0:128]
            for h in range(1, chunk // 128):
                part = part + e[:, h * 128:(h + 1) * 128]
            rs_scr[...] += part
            return carry

        lax.fori_loop(0, nchunks, pass1, 0)
        rowsum = jnp.sum(rs_scr[...], axis=1, keepdims=True)
        qf = q.astype(jnp.float32)
        skf = sk_ref[...].astype(jnp.float32)
        qpos = off_ref[0] + q0 + qi
        sink_e = []
        for j in range(SINKS):
            sj = jnp.sum(qf * skf[j:j + 1, :], axis=1, keepdims=True)
            tj = 50.0 * jnp.tanh(sj * (1.0 / 600.0))
            sink_e.append(jnp.where(qpos >= j, jnp.exp(tj), 0.0))
        ssum = sink_e[0]
        for j in range(1, SINKS):
            ssum = ssum + sink_e[j]
        total = rowsum + ssum
        inv = 1.0 / total
        acc_scr[...] = jnp.zeros((rows, HEAD), jnp.float32)

        def pass2(c, carry):
            start = pl.multiple_of(q0 + c * chunk, chunk)
            w = (expo_scr[c] * inv).astype(jnp.bfloat16)
            vc = v_ref[pl.ds(start, chunk), :]
            acc_scr[...] += jnp.dot(w, vc, preferred_element_type=jnp.float32)
            return carry

        lax.fori_loop(0, nchunks, pass2, 0)
        out = acc_scr[...]
        svf = sv_ref[...].astype(jnp.float32)
        for j in range(SINKS):
            wj = (sink_e[j] * inv).astype(jnp.bfloat16).astype(jnp.float32)
            out = out + wj * svf[j:j + 1, :]
        out16 = out.astype(jnp.bfloat16)
        for g in range(group):
            o_ref[:, g * HEAD:(g + 1) * HEAD] = out16[g * tq:(g + 1) * tq]
            ss_ref[0, g] = ssum[g * tq:(g + 1) * tq]

    off = jnp.reshape(offset, (1,)).astype(jnp.int32)
    return pl.pallas_call(
        kernel,
        out_shape=(
            jax.ShapeDtypeStruct((tok_rows, local_kv * group * HEAD), jnp.bfloat16),
            jax.ShapeDtypeStruct((local_kv, group, tok_rows, 1), jnp.float32),
        ),
        grid_spec=pltpu.PrefetchScalarGridSpec(
            num_scalar_prefetch=1,
            grid=(local_kv, n_qt),
            in_specs=[
                pl.BlockSpec((tq, group * HEAD), lambda k, i, o: (i, k)),
                pl.BlockSpec((span, HEAD), lambda k, i, o: (0, k)),
                pl.BlockSpec((span, HEAD), lambda k, i, o: (0, local_kv + k)),
                pl.BlockSpec((SINKS, HEAD), lambda k, i, o: (0, k)),
                pl.BlockSpec((SINKS, HEAD), lambda k, i, o: (0, local_kv + k)),
            ],
            out_specs=[
                pl.BlockSpec((tq, group * HEAD), lambda k, i, o: (i, k)),
                pl.BlockSpec((1, group, tq, 1), lambda k, i, o: (k, 0, i, 0)),
            ],
            scratch_shapes=[
                pltpu.VMEM((nchunks, rows, chunk), jnp.float32),
                pltpu.VMEM((rows, HEAD), jnp.float32),
                pltpu.VMEM((rows, 128), jnp.float32),
            ],
        ),
        compiler_params=pltpu.CompilerParams(dimension_semantics=("arbitrary", "arbitrary")),
    )(off, query2d, kv_all, kv_all, sink_kv, sink_kv)


def on_device(hidden_in, pre_gain, w_query, w_key, w_value, w_out, post_gain):
    tok_rows = hidden_in.shape[0]
    local_q = w_query.shape[1] // HEAD
    local_kv = w_key.shape[1] // HEAD
    group = local_q // local_kv
    kv_cols = local_kv * HEAD
    tp_n = lax.axis_size("tp")
    tp_i = lax.axis_index("tp")
    cols_dev = post_gain.shape[0]

    w_blocks = w_out.reshape(w_out.shape[0], tp_n, cols_dev)
    w_recv = []
    for k in range(tp_n):
        part = lax.dynamic_index_in_dim(w_blocks, (tp_i + k) % tp_n, axis=1, keepdims=False)
        w_recv.append(part if k == 0 else cyclic(part, "tp", k))

    offset = lax.axis_index("ctx") * tok_rows
    inputs = hidden_in.astype(jnp.float32)
    normed = (
        inputs * lax.rsqrt(jnp.mean(inputs * inputs, axis=-1, keepdims=True) + 1e-06) * pre_gain
    ).astype(jnp.bfloat16)
    positions = offset + jnp.arange(tok_rows, dtype=jnp.int32)
    cosine_table, sine_table = rope_tables(positions)
    query = jnp.dot(normed, w_query, preferred_element_type=jnp.float32).reshape(
        tok_rows, local_q, HEAD
    )
    query = (
        rotate(query, cosine_table, sine_table)
        .astype(jnp.bfloat16)
        .reshape(tok_rows, local_kv, group, HEAD)
    )
    keys = jnp.dot(normed, w_key, preferred_element_type=jnp.float32).reshape(tok_rows, -1, HEAD)
    keys = rotate(keys, cosine_table, sine_table).astype(jnp.bfloat16).reshape(tok_rows, -1)
    values = jnp.dot(normed, w_value, preferred_element_type=jnp.float32).astype(jnp.bfloat16)
    kv = jnp.concatenate([keys, values], axis=1)

    sink_kv = lax.all_gather(kv[:SINKS], "ctx")[0]
    reach = WINDOW // tok_rows
    pieces = [shifted(kv, "ctx", distance) for distance in range(reach, 0, -1)]
    kv_all = jnp.concatenate(pieces + [kv], axis=0)
    attended, sink_parts = window_attention(query.reshape(tok_rows, -1), kv_all, sink_kv, offset, local_kv, group)
    sink_sums = jnp.sum(sink_parts[..., 0], axis=(0, 1))

    projected = jnp.dot(attended, w_recv[0], preferred_element_type=jnp.float32)
    for k in range(1, tp_n):
        projected = projected + jnp.dot(
            cyclic(attended, "tp", k), w_recv[k], preferred_element_type=jnp.float32
        )
    squares = jnp.sum(projected * projected, axis=-1)
    total_squares, total_sinks = lax.psum((squares, sink_sums), "tp")
    post = projected * lax.rsqrt(total_squares / D + 1e-06)[:, None] * post_gain
    own_cols = lax.dynamic_slice_in_dim(inputs, tp_i * cols_dev, cols_dev, 1)
    layer_out = (own_cols + post).astype(jnp.bfloat16)
    sink_share = jnp.log(total_sinks / QHEADS)
    return (layer_out, sink_share)


def solution(mesh):
    return jax.shard_map(
        on_device,
        mesh=mesh,
        in_specs=(
            P("ctx", None),
            P(),
            P(None, "tp"),
            P(None, "tp"),
            P(None, "tp"),
            P("tp", None),
            P("tp"),
        ),
        out_specs=(P("ctx", "tp"), P("ctx")),
        check_vma=False,
    )
```

```python
import math

import jax
import jax.numpy as jnp
from jax import lax
from jax.experimental import pallas as pl
from jax.experimental.pallas import tpu as pltpu
from jax.sharding import PartitionSpec as P

D = 4608
QHEADS = 16
HEAD = 128
WINDOW = 4096
SINKS = 4
EXP_SCALE = 50.0 / math.log(2.0)


def shifted(x, axis, by):
    devices = lax.axis_size(axis)
    pairs = [(i, i + by) for i in range(devices) if 0 <= i + by < devices]
    return lax.ppermute(x, axis, pairs)


def cyclic(x, axis, by):
    devices = lax.axis_size(axis)
    return lax.ppermute(x, axis, [(i, (i + by) % devices) for i in range(devices)])


def rope_tables(positions):
    index = jnp.arange(0, HEAD, 2).astype(jnp.float32)
    inverse = jnp.exp(-jnp.log(jnp.float32(10000.0)) * index / HEAD)
    angles = positions.astype(jnp.float32)[:, None] * inverse[None, :]
    angles = jnp.concatenate([angles, angles], axis=1)
    return (jnp.cos(angles)[:, None, :], jnp.sin(angles)[:, None, :])


def rotate(values, cosine_table, sine_table):
    half = values.shape[-1] // 2
    turned = jnp.concatenate([-values[..., half:], values[..., :half]], axis=-1)
    return values * cosine_table + turned * sine_table


def window_attention(query2d, kv_all, sink_pad, offset, local_kv, group, extra=(), tq=256, chunk=256):
    tok_rows = query2d.shape[0]
    span = kv_all.shape[0]
    rows = group * tq
    win = WINDOW + tq
    nchunks = win // chunk
    n_qt = tok_rows // tq
    pad_rows = sink_pad.shape[0]

    def kernel(off_ref, q_ref, k_ref, v_ref, sk_ref, sv_ref, *rest):
        o_ref, ss_ref, expo_scr, acc_scr, rs_scr = rest[len(extra):]
        i = pl.program_id(1)
        q0 = i * tq
        base = off_ref[0] - WINDOW + q0
        qb = q_ref[...]
        q = jnp.concatenate([qb[:, g * HEAD:(g + 1) * HEAD] for g in range(group)], axis=0)
        qi = lax.broadcasted_iota(jnp.int32, (rows, 1), 0) % tq
        lo = jnp.maximum(qi + 1, SINKS - base)
        hi = qi + WINDOW
        first = jnp.maximum(SINKS - base, 0) // chunk
        rs_scr[...] = jnp.zeros((rows, 128), jnp.float32)

        def keep(c, e):
            expo_scr[c] = e
            part = e[:, 0:128]
            for h in range(1, chunk // 128):
                part = part + e[:, h * 128:(h + 1) * 128]
            rs_scr[...] += part

        def pass1(c, carry):
            start = pl.multiple_of(q0 + c * chunk, chunk)
            kc = k_ref[pl.ds(start, chunk), :]
            s = lax.dot_general(q, kc, (((1,), (1,)), ((), ())), preferred_element_type=jnp.float32)
            u = jnp.tanh(s * (1.0 / 600.0))
            edge = (c == 0) | (c == nchunks - 1) | (base + c * chunk < SINKS)

            @pl.when(edge)
            def _():
                col = c * chunk + lax.broadcasted_iota(jnp.int32, (1, chunk), 1)
                live = (col >= lo) & (col <= hi)
                keep(c, jnp.where(live, jnp.exp2(u * EXP_SCALE), 0.0))

            @pl.when(jnp.logical_not(edge))
            def _():
                keep(c, jnp.exp2(u * EXP_SCALE))

            return carry

        lax.fori_loop(first, nchunks, pass1, 0)
        rowsum = jnp.sum(rs_scr[...], axis=1, keepdims=True)
        ssc = lax.dot_general(q, sk_ref[...], (((1,), (1,)), ((), ())), preferred_element_type=jnp.float32)
        su = jnp.tanh(ssc * (1.0 / 600.0))
        scol = lax.broadcasted_iota(jnp.int32, (1, pad_rows), 1)
        qpos = off_ref[0] + q0 + qi
        slive = (scol < SINKS) & (qpos >= scol)
        se = jnp.where(slive, jnp.exp2(su * EXP_SCALE), 0.0)
        ssum = jnp.sum(se, axis=1, keepdims=True)
        total = rowsum + ssum
        inv = 1.0 / total
        sw = (se * inv).astype(jnp.bfloat16)
        acc_scr[...] = jnp.dot(sw, sv_ref[...], preferred_element_type=jnp.float32)

        def pass2(c, carry):
            start = pl.multiple_of(q0 + c * chunk, chunk)
            w = (expo_scr[c] * inv).astype(jnp.bfloat16)
            vc = v_ref[pl.ds(start, chunk), :]
            acc_scr[...] += jnp.dot(w, vc, preferred_element_type=jnp.float32)
            return carry

        lax.fori_loop(first, nchunks, pass2, 0)
        out16 = acc_scr[...].astype(jnp.bfloat16)
        for g in range(group):
            o_ref[:, g * HEAD:(g + 1) * HEAD] = out16[g * tq:(g + 1) * tq]
            ss_ref[0, g] = ssum[g * tq:(g + 1) * tq]

    off = jnp.reshape(offset, (1,)).astype(jnp.int32)
    return pl.pallas_call(
        kernel,
        out_shape=(
            jax.ShapeDtypeStruct((tok_rows, local_kv * group * HEAD), jnp.bfloat16),
            jax.ShapeDtypeStruct((local_kv, group, tok_rows, 1), jnp.float32),
        ),
        grid_spec=pltpu.PrefetchScalarGridSpec(
            num_scalar_prefetch=1,
            grid=(local_kv, n_qt),
            in_specs=[
                pl.BlockSpec((tq, group * HEAD), lambda k, i, o: (i, k)),
                pl.BlockSpec((span, HEAD), lambda k, i, o: (0, k)),
                pl.BlockSpec((span, HEAD), lambda k, i, o: (0, local_kv + k)),
                pl.BlockSpec((pad_rows, HEAD), lambda k, i, o: (0, k)),
                pl.BlockSpec((pad_rows, HEAD), lambda k, i, o: (0, local_kv + k)),
            ] + [pl.BlockSpec(memory_space=pl.ANY) for _ in extra],
            out_specs=[
                pl.BlockSpec((tq, group * HEAD), lambda k, i, o: (i, k)),
                pl.BlockSpec((1, group, tq, 1), lambda k, i, o: (k, 0, i, 0)),
            ],
            scratch_shapes=[
                pltpu.VMEM((nchunks, rows, chunk), jnp.float32),
                pltpu.VMEM((rows, HEAD), jnp.float32),
                pltpu.VMEM((rows, 128), jnp.float32),
            ],
        ),
        compiler_params=pltpu.CompilerParams(dimension_semantics=("arbitrary", "arbitrary")),
    )(off, query2d, kv_all, kv_all, sink_pad, sink_pad, *extra)


def on_device(hidden_in, pre_gain, w_query, w_key, w_value, w_out, post_gain):
    tok_rows = hidden_in.shape[0]
    local_q = w_query.shape[1] // HEAD
    local_kv = w_key.shape[1] // HEAD
    group = local_q // local_kv
    kv_cols = local_kv * HEAD
    tp_n = lax.axis_size("tp")
    tp_i = lax.axis_index("tp")
    cols_dev = post_gain.shape[0]

    w_blocks = w_out.reshape(w_out.shape[0], tp_n, cols_dev)
    w_recv = []
    for k in range(tp_n):
        part = lax.dynamic_index_in_dim(w_blocks, (tp_i + k) % tp_n, axis=1, keepdims=False)
        w_recv.append(part if k == 0 else cyclic(part, "tp", k))

    offset = lax.axis_index("ctx") * tok_rows
    inputs = hidden_in.astype(jnp.float32)
    normed = (
        inputs * lax.rsqrt(jnp.mean(inputs * inputs, axis=-1, keepdims=True) + 1e-06) * pre_gain
    ).astype(jnp.bfloat16)
    positions = offset + jnp.arange(tok_rows, dtype=jnp.int32)
    cosine_table, sine_table = rope_tables(positions)
    query = jnp.dot(normed, w_query, preferred_element_type=jnp.float32).reshape(
        tok_rows, local_q, HEAD
    )
    query = (
        rotate(query, cosine_table, sine_table)
        .astype(jnp.bfloat16)
        .reshape(tok_rows, local_kv, group, HEAD)
    )
    keys = jnp.dot(normed, w_key, preferred_element_type=jnp.float32).reshape(tok_rows, -1, HEAD)
    keys = rotate(keys, cosine_table, sine_table).astype(jnp.bfloat16).reshape(tok_rows, -1)
    values = jnp.dot(normed, w_value, preferred_element_type=jnp.float32).astype(jnp.bfloat16)
    kv = jnp.concatenate([keys, values], axis=1)

    sink_kv = lax.all_gather(kv[:SINKS], "ctx")[0]
    sink_pad = jnp.zeros((HEAD, sink_kv.shape[1]), sink_kv.dtype).at[:SINKS].set(sink_kv)
    kv_send, sink_pad = lax.optimization_barrier((kv, sink_pad))
    reach = WINDOW // tok_rows
    pieces = [shifted(kv_send, "ctx", distance) for distance in range(reach, 0, -1)]
    kv_all = jnp.concatenate(pieces + [kv], axis=0)
    attended, sink_parts = window_attention(
        query.reshape(tok_rows, -1), kv_all, sink_pad, offset, local_kv, group, extra=tuple(w_recv[1:])
    )
    sink_sums = jnp.sum(sink_parts[..., 0], axis=(0, 1))

    projected = jnp.dot(attended, w_recv[0], preferred_element_type=jnp.float32)
    for k in range(1, tp_n):
        projected = projected + jnp.dot(
            cyclic(attended, "tp", k), w_recv[k], preferred_element_type=jnp.float32
        )
    squares = jnp.sum(projected * projected, axis=-1)
    total_squares, total_sinks = lax.psum((squares, sink_sums), "tp")
    post = projected * lax.rsqrt(total_squares / D + 1e-06)[:, None] * post_gain
    own_cols = lax.dynamic_slice_in_dim(inputs, tp_i * cols_dev, cols_dev, 1)
    layer_out = (own_cols + post).astype(jnp.bfloat16)
    sink_share = jnp.log(total_sinks / QHEADS)
    return (layer_out, sink_share)


def solution(mesh):
    return jax.shard_map(
        on_device,
        mesh=mesh,
        in_specs=(
            P("ctx", None),
            P(),
            P(None, "tp"),
            P(None, "tp"),
            P(None, "tp"),
            P("tp", None),
            P("tp"),
        ),
        out_specs=(P("ctx", "tp"), P("ctx")),
        check_vma=False,
    )
```

```python
import math

import jax
import jax.numpy as jnp
from jax import lax
from jax.experimental import pallas as pl
from jax.experimental.pallas import tpu as pltpu
from jax.sharding import PartitionSpec as P

D = 4608
QHEADS = 16
HEAD = 128
WINDOW = 4096
SINKS = 4
EXP_SCALE = 50.0 / math.log(2.0)


def shifted(x, axis, by):
    devices = lax.axis_size(axis)
    pairs = [(i, i + by) for i in range(devices) if 0 <= i + by < devices]
    return lax.ppermute(x, axis, pairs)


def cyclic(x, axis, by):
    devices = lax.axis_size(axis)
    return lax.ppermute(x, axis, [(i, (i + by) % devices) for i in range(devices)])


def from_first(x, axis):
    devices = lax.axis_size(axis)
    index = lax.axis_index(axis)
    step = devices // 2
    while step >= 1:
        pairs = [(i, i + step) for i in range(0, devices, 2 * step)]
        got = lax.ppermute(x, axis, pairs)
        x = jnp.where(index % (2 * step) == step, got, x)
        step //= 2
    return x


def rope_tables(positions):
    index = jnp.arange(0, HEAD, 2).astype(jnp.float32)
    inverse = jnp.exp(-jnp.log(jnp.float32(10000.0)) * index / HEAD)
    angles = positions.astype(jnp.float32)[:, None] * inverse[None, :]
    angles = jnp.concatenate([angles, angles], axis=1)
    return (jnp.cos(angles)[:, None, :], jnp.sin(angles)[:, None, :])


def rotate(values, cosine_table, sine_table):
    half = values.shape[-1] // 2
    turned = jnp.concatenate([-values[..., half:], values[..., :half]], axis=-1)
    return values * cosine_table + turned * sine_table


def window_attention(query2d, pieces, sink_pad, offset, local_kv, group, extra=(), tq=256, chunk=256):
    tok_rows = query2d.shape[0]
    piece_rows = pieces[0].shape[0]
    n_pieces = len(pieces)
    span = piece_rows * n_pieces
    rows = group * tq
    win = WINDOW + tq
    nchunks = win // chunk
    n_qt = tok_rows // tq
    pad_rows = sink_pad.shape[0]

    def kernel(off_ref, q_ref, sk_ref, sv_ref, *rest):
        piece_refs = rest[:n_pieces]
        o_ref, ss_ref, expo_scr, acc_scr, rs_scr, k_ref, v_ref, sems = rest[n_pieces + len(extra):]
        k = pl.program_id(0)
        i = pl.program_id(1)

        @pl.when(i == 0)
        def _():
            copies = []
            for p in range(n_pieces):
                rows_p = pl.ds(p * piece_rows, piece_rows)
                copies.append(pltpu.make_async_copy(
                    piece_refs[p].at[:, pl.ds(k * HEAD, HEAD)], k_ref.at[rows_p, :], sems.at[0, p]))
                copies.append(pltpu.make_async_copy(
                    piece_refs[p].at[:, pl.ds((local_kv + k) * HEAD, HEAD)], v_ref.at[rows_p, :], sems.at[1, p]))
            for cp in copies:
                cp.start()
            for cp in copies:
                cp.wait()

        q0 = i * tq
        base = off_ref[0] - WINDOW + q0
        qb = q_ref[...]
        q = jnp.concatenate([qb[:, g * HEAD:(g + 1) * HEAD] for g in range(group)], axis=0)
        qi = lax.broadcasted_iota(jnp.int32, (rows, 1), 0) % tq
        lo = jnp.maximum(qi + 1, SINKS - base)
        hi = qi + WINDOW
        first = jnp.maximum(SINKS - base, 0) // chunk
        rs_scr[...] = jnp.zeros((rows, 128), jnp.float32)

        def keep(c, e):
            expo_scr[c] = e
            part = e[:, 0:128]
            for h in range(1, chunk // 128):
                part = part + e[:, h * 128:(h + 1) * 128]
            rs_scr[...] += part

        def pass1(c, carry):
            start = pl.multiple_of(q0 + c * chunk, chunk)
            kc = k_ref[pl.ds(start, chunk), :]
            s = lax.dot_general(q, kc, (((1,), (1,)), ((), ())), preferred_element_type=jnp.float32)
            u = jnp.tanh(s * (1.0 / 600.0))
            edge = (c == 0) | (c == nchunks - 1) | (base + c * chunk < SINKS)

            @pl.when(edge)
            def _():
                col = c * chunk + lax.broadcasted_iota(jnp.int32, (1, chunk), 1)
                live = (col >= lo) & (col <= hi)
                keep(c, jnp.where(live, jnp.exp2(u * EXP_SCALE), 0.0))

            @pl.when(jnp.logical_not(edge))
            def _():
                keep(c, jnp.exp2(u * EXP_SCALE))

            return carry

        lax.fori_loop(first, nchunks, pass1, 0)
        rowsum = jnp.sum(rs_scr[...], axis=1, keepdims=True)
        ssc = lax.dot_general(q, sk_ref[...], (((1,), (1,)), ((), ())), preferred_element_type=jnp.float32)
        su = jnp.tanh(ssc * (1.0 / 600.0))
        scol = lax.broadcasted_iota(jnp.int32, (1, pad_rows), 1)
        qpos = off_ref[0] + q0 + qi
        slive = (scol < SINKS) & (qpos >= scol)
        se = jnp.where(slive, jnp.exp2(su * EXP_SCALE), 0.0)
        ssum = jnp.sum(se, axis=1, keepdims=True)
        total = rowsum + ssum
        inv = 1.0 / total
        sw = (se * inv).astype(jnp.bfloat16)
        acc_scr[...] = jnp.dot(sw, sv_ref[...], preferred_element_type=jnp.float32)

        def pass2(c, carry):
            start = pl.multiple_of(q0 + c * chunk, chunk)
            w = (expo_scr[c] * inv).astype(jnp.bfloat16)
            vc = v_ref[pl.ds(start, chunk), :]
            acc_scr[...] += jnp.dot(w, vc, preferred_element_type=jnp.float32)
            return carry

        lax.fori_loop(first, nchunks, pass2, 0)
        out16 = acc_scr[...].astype(jnp.bfloat16)
        for g in range(group):
            o_ref[:, g * HEAD:(g + 1) * HEAD] = out16[g * tq:(g + 1) * tq]
            ss_ref[0, g] = ssum[g * tq:(g + 1) * tq]

    off = jnp.reshape(offset, (1,)).astype(jnp.int32)
    return pl.pallas_call(
        kernel,
        out_shape=(
            jax.ShapeDtypeStruct((tok_rows, local_kv * group * HEAD), jnp.bfloat16),
            jax.ShapeDtypeStruct((local_kv, group, tok_rows, 1), jnp.float32),
        ),
        grid_spec=pltpu.PrefetchScalarGridSpec(
            num_scalar_prefetch=1,
            grid=(local_kv, n_qt),
            in_specs=[
                pl.BlockSpec((tq, group * HEAD), lambda k, i, o: (i, k)),
                pl.BlockSpec((pad_rows, HEAD), lambda k, i, o: (0, k)),
                pl.BlockSpec((pad_rows, HEAD), lambda k, i, o: (0, local_kv + k)),
            ] + [pl.BlockSpec(memory_space=pl.ANY) for _ in tuple(pieces) + tuple(extra)],
            out_specs=[
                pl.BlockSpec((tq, group * HEAD), lambda k, i, o: (i, k)),
                pl.BlockSpec((1, group, tq, 1), lambda k, i, o: (k, 0, i, 0)),
            ],
            scratch_shapes=[
                pltpu.VMEM((nchunks, rows, chunk), jnp.float32),
                pltpu.VMEM((rows, HEAD), jnp.float32),
                pltpu.VMEM((rows, 128), jnp.float32),
                pltpu.VMEM((span, HEAD), jnp.bfloat16),
                pltpu.VMEM((span, HEAD), jnp.bfloat16),
                pltpu.SemaphoreType.DMA((2, n_pieces)),
            ],
        ),
        compiler_params=pltpu.CompilerParams(dimension_semantics=("arbitrary", "arbitrary")),
    )(off, query2d, sink_pad, sink_pad, *pieces, *extra)


def on_device(hidden_in, pre_gain, w_query, w_key, w_value, w_out, post_gain):
    tok_rows = hidden_in.shape[0]
    local_q = w_query.shape[1] // HEAD
    local_kv = w_key.shape[1] // HEAD
    group = local_q // local_kv
    kv_cols = local_kv * HEAD
    tp_n = lax.axis_size("tp")
    tp_i = lax.axis_index("tp")
    cols_dev = post_gain.shape[0]

    w_blocks = w_out.reshape(w_out.shape[0], tp_n, cols_dev)
    w_recv = []
    for k in range(tp_n):
        part = lax.dynamic_index_in_dim(w_blocks, (tp_i + k) % tp_n, axis=1, keepdims=False)
        w_recv.append(part if k == 0 else cyclic(part, "tp", k))

    offset = lax.axis_index("ctx") * tok_rows
    inputs = hidden_in.astype(jnp.float32)
    normed = (
        inputs * lax.rsqrt(jnp.mean(inputs * inputs, axis=-1, keepdims=True) + 1e-06) * pre_gain
    ).astype(jnp.bfloat16)
    positions = offset + jnp.arange(tok_rows, dtype=jnp.int32)
    cosine_table, sine_table = rope_tables(positions)
    query = jnp.dot(normed, w_query, preferred_element_type=jnp.float32).reshape(
        tok_rows, local_q, HEAD
    )
    query = (
        rotate(query, cosine_table, sine_table)
        .astype(jnp.bfloat16)
        .reshape(tok_rows, local_kv, group, HEAD)
    )
    keys = jnp.dot(normed, w_key, preferred_element_type=jnp.float32).reshape(tok_rows, -1, HEAD)
    keys = rotate(keys, cosine_table, sine_table).astype(jnp.bfloat16).reshape(tok_rows, -1)
    values = jnp.dot(normed, w_value, preferred_element_type=jnp.float32).astype(jnp.bfloat16)
    kv = jnp.concatenate([keys, values], axis=1)

    sink_kv = from_first(kv[:SINKS], "ctx")
    sink_pad = jnp.zeros((HEAD, sink_kv.shape[1]), sink_kv.dtype).at[:SINKS].set(sink_kv)
    reach = WINDOW // tok_rows
    pieces = [shifted(kv, "ctx", distance) for distance in range(reach, 0, -1)] + [kv]
    attended, sink_parts = window_attention(
        query.reshape(tok_rows, -1), pieces, sink_pad, offset, local_kv, group, extra=tuple(w_recv[1:])
    )
    sink_sums = jnp.sum(sink_parts[..., 0], axis=(0, 1))

    projected = jnp.dot(attended, w_recv[0], preferred_element_type=jnp.float32)
    for k in range(1, tp_n):
        projected = projected + jnp.dot(
            cyclic(attended, "tp", k), w_recv[k], preferred_element_type=jnp.float32
        )
    squares = jnp.sum(projected * projected, axis=-1)
    total_squares, total_sinks = lax.psum((squares, sink_sums), "tp")
    post = projected * lax.rsqrt(total_squares / D + 1e-06)[:, None] * post_gain
    own_cols = lax.dynamic_slice_in_dim(hidden_in, tp_i * cols_dev, cols_dev, 1).astype(jnp.float32)
    layer_out = (own_cols + post).astype(jnp.bfloat16)
    sink_share = jnp.log(total_sinks / QHEADS)
    return (layer_out, sink_share)


def solution(mesh):
    return jax.shard_map(
        on_device,
        mesh=mesh,
        in_specs=(
            P("ctx", None),
            P(),
            P(None, "tp"),
            P(None, "tp"),
            P(None, "tp"),
            P("tp", None),
            P("tp"),
        ),
        out_specs=(P("ctx", "tp"), P("ctx")),
        check_vma=False,
    )
```

```python
import math

import jax
import jax.numpy as jnp
from jax import lax
from jax.experimental import pallas as pl
from jax.experimental.pallas import tpu as pltpu
from jax.sharding import PartitionSpec as P

D = 4608
QHEADS = 16
HEAD = 128
WINDOW = 4096
SINKS = 4
EXP_SCALE = 50.0 / math.log(2.0)


def shifted(x, axis, by):
    devices = lax.axis_size(axis)
    pairs = [(i, i + by) for i in range(devices) if 0 <= i + by < devices]
    return lax.ppermute(x, axis, pairs)


def cyclic(x, axis, by):
    devices = lax.axis_size(axis)
    return lax.ppermute(x, axis, [(i, (i + by) % devices) for i in range(devices)])


def from_first(x, axis):
    devices = lax.axis_size(axis)
    index = lax.axis_index(axis)
    step = devices // 2
    while step >= 1:
        pairs = [(i, i + step) for i in range(0, devices, 2 * step)]
        got = lax.ppermute(x, axis, pairs)
        x = jnp.where(index % (2 * step) == step, got, x)
        step //= 2
    return x


def rope_tables(positions):
    index = jnp.arange(0, HEAD, 2).astype(jnp.float32)
    inverse = jnp.exp(-jnp.log(jnp.float32(10000.0)) * index / HEAD)
    angles = positions.astype(jnp.float32)[:, None] * inverse[None, :]
    angles = jnp.concatenate([angles, angles], axis=1)
    return (jnp.cos(angles)[:, None, :], jnp.sin(angles)[:, None, :])


def rotate(values, cosine_table, sine_table):
    half = values.shape[-1] // 2
    turned = jnp.concatenate([-values[..., half:], values[..., :half]], axis=-1)
    return values * cosine_table + turned * sine_table


def window_attention(query, cosine, sine, pieces, sink_pad, offset, local_kv, group, tile, extra=(), tq=256, chunk=256):
    piece_rows = pieces[0].shape[0]
    n_pieces = len(pieces)
    span = piece_rows * n_pieces
    rows = group * tq
    win = WINDOW + tq
    nchunks = win // chunk
    pad_rows = sink_pad.shape[0]

    def kernel(off_ref, q_ref, cos_ref, sin_ref, sk_ref, sv_ref, *rest):
        piece_refs = rest[:n_pieces]
        o_ref, ss_ref, expo_scr, acc_scr, rs_scr, k_ref, v_ref, sems = rest[n_pieces + len(extra):]
        k = pl.program_id(0)
        if True:
            copies = []
            for p in range(n_pieces):
                rows_p = pl.ds(p * piece_rows, piece_rows)
                copies.append(pltpu.make_async_copy(
                    piece_refs[p].at[:, pl.ds(k * HEAD, HEAD)], k_ref.at[rows_p, :], sems.at[0, p]))
                copies.append(pltpu.make_async_copy(
                    piece_refs[p].at[:, pl.ds((local_kv + k) * HEAD, HEAD)], v_ref.at[rows_p, :], sems.at[1, p]))
            for cp in copies:
                cp.start()
            for cp in copies:
                cp.wait()

        q0 = tile * tq
        base = off_ref[0] - WINDOW + q0
        half = lax.broadcasted_iota(jnp.int32, (1, HEAD), 1) < HEAD // 2
        sign = jnp.where(half, -1.0, 1.0).astype(jnp.float32)
        cos_t = cos_ref[...]
        sin_t = sin_ref[...]
        heads = []
        for g in range(group):
            x = q_ref[:, g * HEAD:(g + 1) * HEAD]
            turned = pltpu.roll(x, HEAD // 2, 1) * sign
            heads.append((x * cos_t + turned * sin_t).astype(jnp.bfloat16))
        q = jnp.concatenate(heads, axis=0)
        qi = lax.broadcasted_iota(jnp.int32, (rows, 1), 0) % tq
        lo = jnp.maximum(qi + 1, SINKS - base)
        hi = qi + WINDOW
        first = jnp.maximum(SINKS - base, 0) // chunk
        rs_scr[...] = jnp.zeros((rows, 128), jnp.float32)

        def keep(c, e):
            expo_scr[c] = e
            part = e[:, 0:128]
            for h in range(1, chunk // 128):
                part = part + e[:, h * 128:(h + 1) * 128]
            rs_scr[...] += part

        def pass1(c, carry):
            start = pl.multiple_of(q0 + c * chunk, chunk)
            kc = k_ref[pl.ds(start, chunk), :]
            s = lax.dot_general(q, kc, (((1,), (1,)), ((), ())), preferred_element_type=jnp.float32)
            u = jnp.tanh(s * (1.0 / 600.0))
            edge = (c == 0) | (c == nchunks - 1) | (base + c * chunk < SINKS)

            @pl.when(edge)
            def _():
                col = c * chunk + lax.broadcasted_iota(jnp.int32, (1, chunk), 1)
                live = (col >= lo) & (col <= hi)
                keep(c, jnp.where(live, jnp.exp2(u * EXP_SCALE), 0.0))

            @pl.when(jnp.logical_not(edge))
            def _():
                keep(c, jnp.exp2(u * EXP_SCALE))

            return carry

        lax.fori_loop(first, nchunks, pass1, 0)
        rowsum = jnp.sum(rs_scr[...], axis=1, keepdims=True)
        ssc = lax.dot_general(q, sk_ref[...], (((1,), (1,)), ((), ())), preferred_element_type=jnp.float32)
        su = jnp.tanh(ssc * (1.0 / 600.0))
        scol = lax.broadcasted_iota(jnp.int32, (1, pad_rows), 1)
        qpos = off_ref[0] + q0 + qi
        slive = (scol < SINKS) & (qpos >= scol)
        se = jnp.where(slive, jnp.exp2(su * EXP_SCALE), 0.0)
        ssum = jnp.sum(se, axis=1, keepdims=True)
        total = rowsum + ssum
        inv = 1.0 / total
        sw = (se * inv).astype(jnp.bfloat16)
        acc_scr[...] = jnp.dot(sw, sv_ref[...], preferred_element_type=jnp.float32)

        def pass2(c, carry):
            start = pl.multiple_of(q0 + c * chunk, chunk)
            w = (expo_scr[c] * inv).astype(jnp.bfloat16)
            vc = v_ref[pl.ds(start, chunk), :]
            acc_scr[...] += jnp.dot(w, vc, preferred_element_type=jnp.float32)
            return carry

        lax.fori_loop(first, nchunks, pass2, 0)
        out16 = acc_scr[...].astype(jnp.bfloat16)
        for g in range(group):
            o_ref[:, g * HEAD:(g + 1) * HEAD] = out16[g * tq:(g + 1) * tq]
            ss_ref[0, g] = ssum[g * tq:(g + 1) * tq]

    off = jnp.reshape(offset, (1,)).astype(jnp.int32)
    return pl.pallas_call(
        kernel,
        out_shape=(
            jax.ShapeDtypeStruct((tq, local_kv * group * HEAD), jnp.bfloat16),
            jax.ShapeDtypeStruct((local_kv, group, tq, 1), jnp.float32),
        ),
        grid_spec=pltpu.PrefetchScalarGridSpec(
            num_scalar_prefetch=1,
            grid=(local_kv,),
            in_specs=[
                pl.BlockSpec((tq, group * HEAD), lambda k, o: (tile, k)),
                pl.BlockSpec((tq, HEAD), lambda k, o: (tile, 0)),
                pl.BlockSpec((tq, HEAD), lambda k, o: (tile, 0)),
                pl.BlockSpec((pad_rows, HEAD), lambda k, o: (0, k)),
                pl.BlockSpec((pad_rows, HEAD), lambda k, o: (0, local_kv + k)),
            ] + [pl.BlockSpec(memory_space=pl.ANY) for _ in tuple(pieces) + tuple(extra)],
            out_specs=[
                pl.BlockSpec((tq, group * HEAD), lambda k, o: (0, k)),
                pl.BlockSpec((1, group, tq, 1), lambda k, o: (k, 0, 0, 0)),
            ],
            scratch_shapes=[
                pltpu.VMEM((nchunks, rows, chunk), jnp.float32),
                pltpu.VMEM((rows, HEAD), jnp.float32),
                pltpu.VMEM((rows, 128), jnp.float32),
                pltpu.VMEM((span, HEAD), jnp.bfloat16),
                pltpu.VMEM((span, HEAD), jnp.bfloat16),
                pltpu.SemaphoreType.DMA((2, n_pieces)),
            ],
        ),
        compiler_params=pltpu.CompilerParams(dimension_semantics=("arbitrary",)),
    )(off, query, cosine, sine, sink_pad, sink_pad, *pieces, *extra)


def on_device(hidden_in, pre_gain, w_query, w_key, w_value, w_out, post_gain):
    tok_rows = hidden_in.shape[0]
    local_q = w_query.shape[1] // HEAD
    local_kv = w_key.shape[1] // HEAD
    group = local_q // local_kv
    kv_cols = local_kv * HEAD
    tp_n = lax.axis_size("tp")
    tp_i = lax.axis_index("tp")
    cols_dev = post_gain.shape[0]

    w_blocks = w_out.reshape(w_out.shape[0], tp_n, cols_dev)
    w_recv = []
    for k in range(tp_n):
        part = lax.dynamic_index_in_dim(w_blocks, (tp_i + k) % tp_n, axis=1, keepdims=False)
        w_recv.append(part if k == 0 else cyclic(part, "tp", k))

    offset = lax.axis_index("ctx") * tok_rows
    inputs = hidden_in.astype(jnp.float32)
    normed = (
        inputs * lax.rsqrt(jnp.mean(inputs * inputs, axis=-1, keepdims=True) + 1e-06) * pre_gain
    ).astype(jnp.bfloat16)
    positions = offset + jnp.arange(tok_rows, dtype=jnp.int32)
    cosine_table, sine_table = rope_tables(positions)
    query = jnp.dot(normed, w_query, preferred_element_type=jnp.float32)
    keys = jnp.dot(normed, w_key, preferred_element_type=jnp.float32).reshape(tok_rows, -1, HEAD)
    keys = rotate(keys, cosine_table, sine_table).astype(jnp.bfloat16).reshape(tok_rows, -1)
    values = jnp.dot(normed, w_value, preferred_element_type=jnp.float32).astype(jnp.bfloat16)
    kv = jnp.concatenate([keys, values], axis=1)

    sink_kv = from_first(kv[:SINKS], "ctx")
    sink_pad = jnp.zeros((HEAD, sink_kv.shape[1]), sink_kv.dtype).at[:SINKS].set(sink_kv)
    reach = WINDOW // tok_rows
    pieces = [shifted(kv, "ctx", distance) for distance in range(reach, 0, -1)] + [kv]
    tq = 256
    parts = []
    sink_rows = []
    for tile in range(tok_rows // tq):
        attended, sink_parts = window_attention(
            query, cosine_table[:, 0, :], sine_table[:, 0, :], pieces, sink_pad, offset, local_kv, group,
            tile, extra=tuple(w_recv[1:]) if tile == 0 else (), tq=tq,
        )
        sink_rows.append(jnp.sum(sink_parts[..., 0], axis=(0, 1)))
        part = jnp.dot(attended, w_recv[0], preferred_element_type=jnp.float32)
        for k in range(1, tp_n):
            part = part + jnp.dot(
                cyclic(attended, "tp", k), w_recv[k], preferred_element_type=jnp.float32
            )
        parts.append(part)
    projected = jnp.concatenate(parts, axis=0)
    sink_sums = jnp.concatenate(sink_rows, axis=0)
    squares = jnp.sum(projected * projected, axis=-1)
    total_squares, total_sinks = lax.psum((squares, sink_sums), "tp")
    post = projected * lax.rsqrt(total_squares / D + 1e-06)[:, None] * post_gain
    own_cols = lax.dynamic_slice_in_dim(hidden_in, tp_i * cols_dev, cols_dev, 1).astype(jnp.float32)
    layer_out = (own_cols + post).astype(jnp.bfloat16)
    sink_share = jnp.log(total_sinks / QHEADS)
    return (layer_out, sink_share)


def solution(mesh):
    return jax.shard_map(
        on_device,
        mesh=mesh,
        in_specs=(
            P("ctx", None),
            P(),
            P(None, "tp"),
            P(None, "tp"),
            P(None, "tp"),
            P("tp", None),
            P("tp"),
        ),
        out_specs=(P("ctx", "tp"), P("ctx")),
        check_vma=False,
    )
```

```python
import math

import jax
import jax.numpy as jnp
from jax import lax
from jax.experimental import pallas as pl
from jax.experimental.pallas import tpu as pltpu
from jax.sharding import PartitionSpec as P

D = 4608
QHEADS = 16
HEAD = 128
WINDOW = 4096
SINKS = 4
EXP_SCALE = 50.0 / math.log(2.0)


def shifted(x, axis, by):
    devices = lax.axis_size(axis)
    pairs = [(i, i + by) for i in range(devices) if 0 <= i + by < devices]
    return lax.ppermute(x, axis, pairs)


def cyclic(x, axis, by):
    devices = lax.axis_size(axis)
    return lax.ppermute(x, axis, [(i, (i + by) % devices) for i in range(devices)])


def from_first(x, axis):
    devices = lax.axis_size(axis)
    index = lax.axis_index(axis)
    step = devices // 2
    while step >= 1:
        pairs = [(i, i + step) for i in range(0, devices, 2 * step)]
        got = lax.ppermute(x, axis, pairs)
        x = jnp.where(index % (2 * step) == step, got, x)
        step //= 2
    return x


def rope_tables(positions):
    index = jnp.arange(0, HEAD, 2).astype(jnp.float32)
    inverse = jnp.exp(-jnp.log(jnp.float32(10000.0)) * index / HEAD)
    angles = positions.astype(jnp.float32)[:, None] * inverse[None, :]
    angles = jnp.concatenate([angles, angles], axis=1)
    return (jnp.cos(angles)[:, None, :], jnp.sin(angles)[:, None, :])


def rotate(values, cosine_table, sine_table):
    half = values.shape[-1] // 2
    turned = jnp.concatenate([-values[..., half:], values[..., :half]], axis=-1)
    return values * cosine_table + turned * sine_table


def window_attention(query, cosine, sine, pieces, orders, sink_pad, offset, local_kv, group, extra=(), tq=256, chunk=256):
    tok_rows = query.shape[0]
    n_qt = tok_rows // tq
    piece_rows = pieces[0].shape[0]
    n_pieces = len(pieces)
    span = piece_rows * len(orders[0])
    rows = group * tq
    win = WINDOW + tq
    nchunks = win // chunk
    pad_rows = sink_pad.shape[0]

    def kernel(off_ref, q_ref, cos_ref, sin_ref, sk_ref, sv_ref, *rest):
        piece_refs = rest[:n_pieces]
        o_ref, ss_ref, expo_scr, acc_scr, rs_scr, k_ref, v_ref, sems = rest[n_pieces + len(extra):]
        k = pl.program_id(0)
        i = pl.program_id(1)

        parity = (off_ref[0] // piece_rows) % len(orders)

        def fetch(order):
            copies = []
            for p, src in enumerate(order):
                rows_p = pl.ds(p * piece_rows, piece_rows)
                copies.append(pltpu.make_async_copy(
                    piece_refs[src].at[:, pl.ds(k * HEAD, HEAD)], k_ref.at[rows_p, :], sems.at[0, p]))
                copies.append(pltpu.make_async_copy(
                    piece_refs[src].at[:, pl.ds((local_kv + k) * HEAD, HEAD)], v_ref.at[rows_p, :], sems.at[1, p]))
            for cp in copies:
                cp.start()
            for cp in copies:
                cp.wait()

        for which, order in enumerate(orders):
            pl.when((i == 0) & (parity == which))(lambda order=order: fetch(order))

        q0 = i * tq
        base = off_ref[0] - WINDOW + q0
        half = lax.broadcasted_iota(jnp.int32, (1, HEAD), 1) < HEAD // 2
        sign = jnp.where(half, -1.0, 1.0).astype(jnp.float32)
        cos_t = cos_ref[...]
        sin_t = sin_ref[...]
        heads = []
        for g in range(group):
            x = q_ref[:, g * HEAD:(g + 1) * HEAD]
            turned = pltpu.roll(x, HEAD // 2, 1) * sign
            heads.append((x * cos_t + turned * sin_t).astype(jnp.bfloat16))
        q = jnp.concatenate(heads, axis=0)
        qi = lax.broadcasted_iota(jnp.int32, (rows, 1), 0) % tq
        lo = jnp.maximum(qi + 1, SINKS - base)
        hi = qi + WINDOW
        first = jnp.maximum(SINKS - base, 0) // chunk
        rs_scr[...] = jnp.zeros((rows, 128), jnp.float32)

        def keep(c, e):
            expo_scr[c] = e
            part = e[:, 0:128]
            for h in range(1, chunk // 128):
                part = part + e[:, h * 128:(h + 1) * 128]
            rs_scr[...] += part

        def pass1(c, carry):
            start = pl.multiple_of(q0 + c * chunk, chunk)
            kc = k_ref[pl.ds(start, chunk), :]
            s = lax.dot_general(q, kc, (((1,), (1,)), ((), ())), preferred_element_type=jnp.float32)
            u = jnp.tanh(s * (1.0 / 600.0))
            edge = (c * chunk < tq) | ((c + 1) * chunk > WINDOW + 1) | (base + c * chunk < SINKS)

            @pl.when(edge)
            def _():
                col = c * chunk + lax.broadcasted_iota(jnp.int32, (1, chunk), 1)
                live = (col >= lo) & (col <= hi)
                keep(c, jnp.where(live, jnp.exp2(u * EXP_SCALE), 0.0))

            @pl.when(jnp.logical_not(edge))
            def _():
                keep(c, jnp.exp2(u * EXP_SCALE))

            return carry

        lax.fori_loop(first, nchunks, pass1, 0)
        rowsum = jnp.sum(rs_scr[...], axis=1, keepdims=True)
        ssc = lax.dot_general(q, sk_ref[...], (((1,), (1,)), ((), ())), preferred_element_type=jnp.float32)
        su = jnp.tanh(ssc * (1.0 / 600.0))
        scol = lax.broadcasted_iota(jnp.int32, (1, pad_rows), 1)
        qpos = off_ref[0] + q0 + qi
        slive = (scol < SINKS) & (qpos >= scol)
        se = jnp.where(slive, jnp.exp2(su * EXP_SCALE), 0.0)
        ssum = jnp.sum(se, axis=1, keepdims=True)
        total = rowsum + ssum
        inv = 1.0 / total
        sw = (se * inv).astype(jnp.bfloat16)
        acc_scr[...] = jnp.dot(sw, sv_ref[...], preferred_element_type=jnp.float32)

        def pass2(c, carry):
            start = pl.multiple_of(q0 + c * chunk, chunk)
            w = (expo_scr[c] * inv).astype(jnp.bfloat16)
            vc = v_ref[pl.ds(start, chunk), :]
            acc_scr[...] += jnp.dot(w, vc, preferred_element_type=jnp.float32)
            return carry

        lax.fori_loop(first, nchunks, pass2, 0)
        out16 = acc_scr[...].astype(jnp.bfloat16)
        for g in range(group):
            o_ref[:, g * HEAD:(g + 1) * HEAD] = out16[g * tq:(g + 1) * tq]
            ss_ref[0, g] = ssum[g * tq:(g + 1) * tq]

    off = jnp.reshape(offset, (1,)).astype(jnp.int32)
    return pl.pallas_call(
        kernel,
        out_shape=(
            jax.ShapeDtypeStruct((tok_rows, local_kv * group * HEAD), jnp.bfloat16),
            jax.ShapeDtypeStruct((local_kv, group, tok_rows, 1), jnp.float32),
        ),
        grid_spec=pltpu.PrefetchScalarGridSpec(
            num_scalar_prefetch=1,
            grid=(local_kv, n_qt),
            in_specs=[
                pl.BlockSpec((tq, group * HEAD), lambda k, i, o: (i, k)),
                pl.BlockSpec((tq, HEAD), lambda k, i, o: (i, 0)),
                pl.BlockSpec((tq, HEAD), lambda k, i, o: (i, 0)),
                pl.BlockSpec((pad_rows, HEAD), lambda k, i, o: (0, k)),
                pl.BlockSpec((pad_rows, HEAD), lambda k, i, o: (0, local_kv + k)),
            ] + [pl.BlockSpec(memory_space=pl.ANY) for _ in tuple(pieces) + tuple(extra)],
            out_specs=[
                pl.BlockSpec((tq, group * HEAD), lambda k, i, o: (i, k)),
                pl.BlockSpec((1, group, tq, 1), lambda k, i, o: (k, 0, i, 0)),
            ],
            scratch_shapes=[
                pltpu.VMEM((nchunks, rows, chunk), jnp.float32),
                pltpu.VMEM((rows, HEAD), jnp.float32),
                pltpu.VMEM((rows, 128), jnp.float32),
                pltpu.VMEM((span, HEAD), jnp.bfloat16),
                pltpu.VMEM((span, HEAD), jnp.bfloat16),
                pltpu.SemaphoreType.DMA((2, len(orders[0]))),
            ],
        ),
        compiler_params=pltpu.CompilerParams(dimension_semantics=("arbitrary", "arbitrary")),
    )(off, query, cosine, sine, sink_pad, sink_pad, *pieces, *extra)


def on_device(hidden_in, pre_gain, w_query, w_key, w_value, w_out, post_gain):
    tok_rows = hidden_in.shape[0]
    local_q = w_query.shape[1] // HEAD
    local_kv = w_key.shape[1] // HEAD
    group = local_q // local_kv
    kv_cols = local_kv * HEAD
    tp_n = lax.axis_size("tp")
    tp_i = lax.axis_index("tp")
    cols_dev = post_gain.shape[0]

    w_blocks = w_out.reshape(w_out.shape[0], tp_n, cols_dev)
    w_recv = []
    for k in range(tp_n):
        part = lax.dynamic_index_in_dim(w_blocks, (tp_i + k) % tp_n, axis=1, keepdims=False)
        w_recv.append(part if k == 0 else cyclic(part, "tp", k))

    offset = lax.axis_index("ctx") * tok_rows
    inputs = hidden_in.astype(jnp.float32)
    normed = (
        inputs * lax.rsqrt(jnp.mean(inputs * inputs, axis=-1, keepdims=True) + 1e-06) * pre_gain
    ).astype(jnp.bfloat16)
    positions = offset + jnp.arange(tok_rows, dtype=jnp.int32)
    cosine_table, sine_table = rope_tables(positions)
    query = jnp.dot(normed, w_query, preferred_element_type=jnp.float32)
    keys = jnp.dot(normed, w_key, preferred_element_type=jnp.float32).reshape(tok_rows, -1, HEAD)
    keys = rotate(keys, cosine_table, sine_table).astype(jnp.bfloat16).reshape(tok_rows, -1)
    values = jnp.dot(normed, w_value, preferred_element_type=jnp.float32).astype(jnp.bfloat16)
    kv = jnp.concatenate([keys, values], axis=1)

    sink_kv = from_first(kv[:SINKS], "ctx")
    sink_pad = jnp.zeros((HEAD, sink_kv.shape[1]), sink_kv.dtype).at[:SINKS].set(sink_kv)
    reach = WINDOW // tok_rows
    ctx_n = lax.axis_size("ctx")
    fetched = [shifted(kv, "ctx", distance) for distance in range(reach, 0, -2)]
    swapped = lax.ppermute(jnp.stack(fetched + [kv]), "ctx", [(i, i ^ 1) for i in range(ctx_n)])
    pieces = fetched + [swapped[j] for j in range(len(fetched) + 1)] + [kv]
    own = len(pieces) - 1
    half = len(fetched)
    even_order, odd_order = [], []
    for j in range(half):
        even_order += [j, half + j]
        odd_order += [j, half + j + 1]
    orders = (tuple(even_order + [own]), tuple(odd_order + [own]))
    attended, sink_parts = window_attention(
        query, cosine_table[:, 0, :], sine_table[:, 0, :], pieces, orders, sink_pad, offset, local_kv, group,
        extra=tuple(w_recv[1:]),
    )
    sink_sums = jnp.sum(sink_parts[..., 0], axis=(0, 1))
    projected = jnp.dot(attended, w_recv[0], preferred_element_type=jnp.float32)
    for k in range(1, tp_n):
        projected = projected + jnp.dot(
            cyclic(attended, "tp", k), w_recv[k], preferred_element_type=jnp.float32
        )
    squares = jnp.sum(projected * projected, axis=-1)
    total_squares, total_sinks = lax.psum((squares, sink_sums), "tp")
    post = projected * lax.rsqrt(total_squares / D + 1e-06)[:, None] * post_gain
    own_cols = lax.dynamic_slice_in_dim(hidden_in, tp_i * cols_dev, cols_dev, 1).astype(jnp.float32)
    layer_out = (own_cols + post).astype(jnp.bfloat16)
    sink_share = jnp.log(total_sinks / QHEADS)
    return (layer_out, sink_share)


def solution(mesh):
    return jax.shard_map(
        on_device,
        mesh=mesh,
        in_specs=(
            P("ctx", None),
            P(),
            P(None, "tp"),
            P(None, "tp"),
            P(None, "tp"),
            P("tp", None),
            P("tp"),
        ),
        out_specs=(P("ctx", "tp"), P("ctx")),
        check_vma=False,
    )
```

```python
import math

import jax
import jax.numpy as jnp
from jax import lax
from jax.experimental import pallas as pl
from jax.experimental.pallas import tpu as pltpu
from jax.sharding import PartitionSpec as P


D = 4608
QHEADS = 16
HEAD = 128
WINDOW = 4096
SINKS = 4
EXP_SCALE = 50.0 / math.log(2.0)


def shifted(x, axis, by):
    devices = lax.axis_size(axis)
    pairs = [(i, i + by) for i in range(devices) if 0 <= i + by < devices]
    return lax.ppermute(x, axis, pairs)


def cyclic(x, axis, by):
    devices = lax.axis_size(axis)
    return lax.ppermute(x, axis, [(i, (i + by) % devices) for i in range(devices)])


def from_first(x, axis):
    devices = lax.axis_size(axis)
    index = lax.axis_index(axis)
    step = devices // 2
    while step >= 1:
        pairs = [(i, i + step) for i in range(0, devices, 2 * step)]
        got = lax.ppermute(x, axis, pairs)
        x = jnp.where(index % (2 * step) == step, got, x)
        step //= 2
    return x


def rope_tables(positions):
    index = jnp.arange(0, HEAD, 2).astype(jnp.float32)
    inverse = jnp.exp(-jnp.log(jnp.float32(10000.0)) * index / HEAD)
    angles = positions.astype(jnp.float32)[:, None] * inverse[None, :]
    angles = jnp.concatenate([angles, angles], axis=1)
    return (jnp.cos(angles)[:, None, :], jnp.sin(angles)[:, None, :])


def rotate(values, cosine_table, sine_table):
    half = values.shape[-1] // 2
    turned = jnp.concatenate([-values[..., half:], values[..., :half]], axis=-1)
    return values * cosine_table + turned * sine_table


def window_attention(query, cosine, sine, pieces, orders, sink_pad, offset, local_kv, group, extra=(), tq=256, chunk=256):
    tok_rows = query.shape[0]
    n_qt = tok_rows // tq
    piece_rows = pieces[0].shape[0]
    n_pieces = len(pieces)
    span = piece_rows * len(orders[0])
    rows = group * tq
    win = WINDOW + tq
    nchunks = win // chunk
    pad_rows = sink_pad.shape[0]

    def kernel(off_ref, q_ref, cos_ref, sin_ref, sk_ref, sv_ref, *rest):
        piece_refs = rest[:n_pieces]
        o_ref, ss_ref, expo_scr, acc_scr, rs_scr, k_ref, v_ref, sems = rest[n_pieces + len(extra):]
        k = pl.program_id(0)
        i = pl.program_id(1)

        parity = (off_ref[0] // piece_rows) % len(orders)

        def fetch(order):
            copies = []
            for p, src in enumerate(order):
                rows_p = pl.ds(p * piece_rows, piece_rows)
                copies.append(pltpu.make_async_copy(
                    piece_refs[src].at[:, pl.ds(k * HEAD, HEAD)], k_ref.at[rows_p, :], sems.at[0, p]))
                copies.append(pltpu.make_async_copy(
                    piece_refs[src].at[:, pl.ds((local_kv + k) * HEAD, HEAD)], v_ref.at[rows_p, :], sems.at[1, p]))
            for cp in copies:
                cp.start()
            for cp in copies:
                cp.wait()

        for which, order in enumerate(orders):
            pl.when((i == 0) & (parity == which))(lambda order=order: fetch(order))

        q0 = i * tq
        base = off_ref[0] - WINDOW + q0
        half = lax.broadcasted_iota(jnp.int32, (1, HEAD), 1) < HEAD // 2
        sign = jnp.where(half, -1.0, 1.0).astype(jnp.float32)
        cos_t = cos_ref[...]
        sin_t = sin_ref[...]
        heads = []
        for g in range(group):
            x = q_ref[:, g * HEAD:(g + 1) * HEAD]
            turned = pltpu.roll(x, HEAD // 2, 1) * sign
            heads.append((x * cos_t + turned * sin_t).astype(jnp.bfloat16))
        q = jnp.concatenate(heads, axis=0)
        qi = lax.broadcasted_iota(jnp.int32, (rows, 1), 0) % tq
        lo = jnp.maximum(qi + 1, SINKS - base)
        hi = qi + WINDOW
        first = jnp.maximum(SINKS - base, 0) // chunk
        rs_scr[...] = jnp.zeros((rows, 128), jnp.float32)

        def keep(c, e):
            expo_scr[c] = e
            part = e[:, 0:128]
            for h in range(1, chunk // 128):
                part = part + e[:, h * 128:(h + 1) * 128]
            rs_scr[...] += part

        def pass1(c, carry):
            start = pl.multiple_of(q0 + c * chunk, chunk)
            kc = k_ref[pl.ds(start, chunk), :]
            s = lax.dot_general(q, kc, (((1,), (1,)), ((), ())), preferred_element_type=jnp.float32)
            u = jnp.tanh(s * (1.0 / 600.0))
            edge = (c * chunk < tq) | ((c + 1) * chunk > WINDOW + 1) | (base + c * chunk < SINKS)

            @pl.when(edge)
            def _():
                col = c * chunk + lax.broadcasted_iota(jnp.int32, (1, chunk), 1)
                live = (col >= lo) & (col <= hi)
                keep(c, jnp.where(live, jnp.exp2(u * EXP_SCALE), 0.0))

            @pl.when(jnp.logical_not(edge))
            def _():
                keep(c, jnp.exp2(u * EXP_SCALE))

            return carry

        lax.fori_loop(first, nchunks, pass1, 0)
        rowsum = jnp.sum(rs_scr[...], axis=1, keepdims=True)
        ssc = lax.dot_general(q, sk_ref[...], (((1,), (1,)), ((), ())), preferred_element_type=jnp.float32)
        su = jnp.tanh(ssc * (1.0 / 600.0))
        scol = lax.broadcasted_iota(jnp.int32, (1, pad_rows), 1)
        qpos = off_ref[0] + q0 + qi
        slive = (scol < SINKS) & (qpos >= scol)
        se = jnp.where(slive, jnp.exp2(su * EXP_SCALE), 0.0)
        ssum = jnp.sum(se, axis=1, keepdims=True)
        total = rowsum + ssum
        inv = 1.0 / total
        sw = (se * inv).astype(jnp.bfloat16)
        acc_scr[...] = jnp.dot(sw, sv_ref[...], preferred_element_type=jnp.float32)

        def pass2(c, carry):
            start = pl.multiple_of(q0 + c * chunk, chunk)
            w = (expo_scr[c] * inv).astype(jnp.bfloat16)
            vc = v_ref[pl.ds(start, chunk), :]
            acc_scr[...] += jnp.dot(w, vc, preferred_element_type=jnp.float32)
            return carry

        lax.fori_loop(first, nchunks, pass2, 0)
        out16 = acc_scr[...].astype(jnp.bfloat16)
        for g in range(group):
            o_ref[:, g * HEAD:(g + 1) * HEAD] = out16[g * tq:(g + 1) * tq]
            ss_ref[0, g] = ssum[g * tq:(g + 1) * tq]

    off = jnp.reshape(offset, (1,)).astype(jnp.int32)
    return pl.pallas_call(
        kernel,
        out_shape=(
            jax.ShapeDtypeStruct((tok_rows, local_kv * group * HEAD), jnp.bfloat16),
            jax.ShapeDtypeStruct((local_kv, group, tok_rows, 1), jnp.float32),
        ),
        grid_spec=pltpu.PrefetchScalarGridSpec(
            num_scalar_prefetch=1,
            grid=(local_kv, n_qt),
            in_specs=[
                pl.BlockSpec((tq, group * HEAD), lambda k, i, o: (i, k)),
                pl.BlockSpec((tq, HEAD), lambda k, i, o: (i, 0)),
                pl.BlockSpec((tq, HEAD), lambda k, i, o: (i, 0)),
                pl.BlockSpec((pad_rows, HEAD), lambda k, i, o: (0, k)),
                pl.BlockSpec((pad_rows, HEAD), lambda k, i, o: (0, local_kv + k)),
            ] + [pl.BlockSpec(memory_space=pl.ANY) for _ in tuple(pieces) + tuple(extra)],
            out_specs=[
                pl.BlockSpec((tq, group * HEAD), lambda k, i, o: (i, k)),
                pl.BlockSpec((1, group, tq, 1), lambda k, i, o: (k, 0, i, 0)),
            ],
            scratch_shapes=[
                pltpu.VMEM((nchunks, rows, chunk), jnp.float32),
                pltpu.VMEM((rows, HEAD), jnp.float32),
                pltpu.VMEM((rows, 128), jnp.float32),
                pltpu.VMEM((span, HEAD), jnp.bfloat16),
                pltpu.VMEM((span, HEAD), jnp.bfloat16),
                pltpu.SemaphoreType.DMA((2, len(orders[0]))),
            ],
        ),
        compiler_params=pltpu.CompilerParams(dimension_semantics=("arbitrary", "arbitrary")),
    )(off, query, cosine, sine, sink_pad, sink_pad, *pieces, *extra)


def on_device(hidden_in, pre_gain, w_query, w_key, w_value, w_out, post_gain):
    tok_rows = hidden_in.shape[0]
    local_q = w_query.shape[1] // HEAD
    local_kv = w_key.shape[1] // HEAD
    group = local_q // local_kv
    tp_n = lax.axis_size("tp")
    tp_i = lax.axis_index("tp")
    cols_dev = post_gain.shape[0]

    w_blocks = w_out.reshape(w_out.shape[0], tp_n, cols_dev)
    w_recv = []
    for k in range(tp_n):
        part = lax.dynamic_index_in_dim(w_blocks, (tp_i + k) % tp_n, axis=1, keepdims=False)
        w_recv.append(part if k == 0 else cyclic(part, "tp", k))

    offset = lax.axis_index("ctx") * tok_rows
    inputs = hidden_in.astype(jnp.float32)
    normed = (
        inputs * lax.rsqrt(jnp.mean(inputs * inputs, axis=-1, keepdims=True) + 1e-06) * pre_gain
    ).astype(jnp.bfloat16)
    positions = offset + jnp.arange(tok_rows, dtype=jnp.int32)
    cosine_table, sine_table = rope_tables(positions)
    query = jnp.dot(normed, w_query, preferred_element_type=jnp.float32)
    keys = jnp.dot(normed, w_key, preferred_element_type=jnp.float32).reshape(tok_rows, -1, HEAD)
    keys = rotate(keys, cosine_table, sine_table).astype(jnp.bfloat16).reshape(tok_rows, -1)
    values = jnp.dot(normed, w_value, preferred_element_type=jnp.float32).astype(jnp.bfloat16)
    kv = jnp.concatenate([keys, values], axis=1)

    sink_kv = from_first(kv[:SINKS], "ctx")
    sink_pad = jnp.zeros((HEAD, sink_kv.shape[1]), sink_kv.dtype).at[:SINKS].set(sink_kv)
    reach = WINDOW // tok_rows
    pieces = [shifted(kv, "ctx", distance) for distance in range(reach, 0, -1)] + [kv]
    orders = (tuple(range(len(pieces))),)
    attended, sink_parts = window_attention(
        query, cosine_table[:, 0, :], sine_table[:, 0, :], pieces, orders, sink_pad, offset, local_kv, group,
        extra=tuple(w_recv[1:]),
    )
    sink_sums = jnp.sum(sink_parts[..., 0], axis=(0, 1))
    projected = jnp.dot(attended, w_recv[0], preferred_element_type=jnp.float32)
    for k in range(1, tp_n):
        projected = projected + jnp.dot(
            cyclic(attended, "tp", k), w_recv[k], preferred_element_type=jnp.float32
        )
    squares = jnp.sum(projected * projected, axis=-1)
    total_squares, total_sinks = lax.psum((squares, sink_sums), "tp")
    post = projected * lax.rsqrt(total_squares / D + 1e-06)[:, None] * post_gain
    own_cols = lax.dynamic_slice_in_dim(hidden_in, tp_i * cols_dev, cols_dev, 1).astype(jnp.float32)
    layer_out = (own_cols + post).astype(jnp.bfloat16)
    sink_share = jnp.log(total_sinks / QHEADS)
    return (layer_out, sink_share)


def solution(mesh):
    return jax.shard_map(
        on_device,
        mesh=mesh,
        in_specs=(
            P("ctx", None),
            P(),
            P(None, "tp"),
            P(None, "tp"),
            P(None, "tp"),
            P("tp", None),
            P("tp"),
        ),
        out_specs=(P("ctx", "tp"), P("ctx")),
        check_vma=False,
    )
```

```python
import math

import jax
import jax.numpy as jnp
from jax import lax
from jax.experimental import pallas as pl
from jax.experimental.pallas import tpu as pltpu
from jax.sharding import PartitionSpec as P


D = 4608
QHEADS = 16
HEAD = 128
WINDOW = 4096
SINKS = 4
EXP_SCALE = 50.0 / math.log(2.0)


def shifted(x, axis, by):
    devices = lax.axis_size(axis)
    pairs = [(i, i + by) for i in range(devices) if 0 <= i + by < devices]
    return lax.ppermute(x, axis, pairs)


def cyclic(x, axis, by):
    devices = lax.axis_size(axis)
    return lax.ppermute(x, axis, [(i, (i + by) % devices) for i in range(devices)])


def from_first(x, axis):
    devices = lax.axis_size(axis)
    index = lax.axis_index(axis)
    step = devices // 2
    while step >= 1:
        pairs = [(i, i + step) for i in range(0, devices, 2 * step)]
        got = lax.ppermute(x, axis, pairs)
        x = jnp.where(index % (2 * step) == step, got, x)
        step //= 2
    return x


def rope_tables(positions):
    index = jnp.arange(0, HEAD, 2).astype(jnp.float32)
    inverse = jnp.exp(-jnp.log(jnp.float32(10000.0)) * index / HEAD)
    angles = positions.astype(jnp.float32)[:, None] * inverse[None, :]
    angles = jnp.concatenate([angles, angles], axis=1)
    return (jnp.cos(angles)[:, None, :], jnp.sin(angles)[:, None, :])


def rotate(values, cosine_table, sine_table):
    half = values.shape[-1] // 2
    turned = jnp.concatenate([-values[..., half:], values[..., :half]], axis=-1)
    return values * cosine_table + turned * sine_table


def window_attention(query, cosine, sine, pieces, orders, sink_pad, offset, local_kv, group, extra=(), tq=256, chunk=256):
    tok_rows = query.shape[0]
    n_qt = tok_rows // tq
    piece_rows = pieces[0].shape[0]
    n_pieces = len(pieces)
    span = piece_rows * len(orders[0])
    rows = group * tq
    win = WINDOW + tq
    nchunks = win // chunk
    pad_rows = sink_pad.shape[0]

    def kernel(off_ref, q_ref, cos_ref, sin_ref, sk_ref, sv_ref, *rest):
        piece_refs = rest[:n_pieces]
        o_ref, ss_ref, expo_scr, acc_scr, rs_scr, k_ref, v_ref, w_scr, sems = rest[n_pieces + len(extra):]
        k = pl.program_id(0)
        i = pl.program_id(1)

        parity = (off_ref[0] // piece_rows) % len(orders)

        def fetch(order):
            copies = []
            for p, src in enumerate(order):
                rows_p = pl.ds(p * piece_rows, piece_rows)
                copies.append(pltpu.make_async_copy(
                    piece_refs[src].at[:, pl.ds(k * HEAD, HEAD)], k_ref.at[rows_p, :], sems.at[0, p]))
                copies.append(pltpu.make_async_copy(
                    piece_refs[src].at[:, pl.ds((local_kv + k) * HEAD, HEAD)], v_ref.at[rows_p, :], sems.at[1, p]))
            for cp in copies:
                cp.start()
            for cp in copies:
                cp.wait()

        for which, order in enumerate(orders):
            pl.when((i == 0) & (parity == which))(lambda order=order: fetch(order))

        q0 = i * tq
        base = off_ref[0] - WINDOW + q0
        half = lax.broadcasted_iota(jnp.int32, (1, HEAD), 1) < HEAD // 2
        sign = jnp.where(half, -1.0, 1.0).astype(jnp.float32)
        cos_t = cos_ref[...]
        sin_t = sin_ref[...]
        heads = []
        for g in range(group):
            x = q_ref[:, g * HEAD:(g + 1) * HEAD]
            turned = pltpu.roll(x, HEAD // 2, 1) * sign
            heads.append((x * cos_t + turned * sin_t).astype(jnp.bfloat16))
        q = jnp.concatenate(heads, axis=0)
        qi = lax.broadcasted_iota(jnp.int32, (rows, 1), 0) % tq
        lo = jnp.maximum(qi + 1, SINKS - base)
        hi = qi + WINDOW
        first = jnp.maximum(SINKS - base, 0) // chunk
        rs_scr[...] = jnp.zeros((rows, 128), jnp.float32)

        def keep(c, e):
            expo_scr[c] = e
            part = e[:, 0:128]
            for h in range(1, chunk // 128):
                part = part + e[:, h * 128:(h + 1) * 128]
            rs_scr[...] += part

        def squash(c):
            start = pl.multiple_of(q0 + c * chunk, chunk)
            kc = k_ref[pl.ds(start, chunk), :]
            s = lax.dot_general(q, kc, (((1,), (1,)), ((), ())), preferred_element_type=jnp.float32)
            return jnp.tanh(s * (1.0 / 600.0))

        def pass1(c, carry):
            edge = (c * chunk < tq) | ((c + 1) * chunk > WINDOW + 1) | (base + c * chunk < SINKS)

            @pl.when(edge)
            def _():
                u = squash(c)
                col = c * chunk + lax.broadcasted_iota(jnp.int32, (1, chunk), 1)
                live = (col >= lo) & (col <= hi)
                keep(c, jnp.where(live, jnp.exp2(u * EXP_SCALE), 0.0))

            @pl.when(jnp.logical_not(edge))
            def _():
                keep(c, jnp.exp2(squash(c) * EXP_SCALE))

            return carry

        lax.fori_loop(first, nchunks, pass1, 0)
        rowsum = jnp.sum(rs_scr[...], axis=1, keepdims=True)
        ssc = lax.dot_general(q, sk_ref[...], (((1,), (1,)), ((), ())), preferred_element_type=jnp.float32)
        su = jnp.tanh(ssc * (1.0 / 600.0))
        scol = lax.broadcasted_iota(jnp.int32, (1, pad_rows), 1)
        qpos = off_ref[0] + q0 + qi
        slive = (scol < SINKS) & (qpos >= scol)
        se = jnp.where(slive, jnp.exp2(su * EXP_SCALE), 0.0)
        ssum = jnp.sum(se, axis=1, keepdims=True)
        total = rowsum + ssum
        inv = 1.0 / total
        sw = (se * inv).astype(jnp.bfloat16)
        acc_scr[...] = jnp.dot(sw, sv_ref[...], preferred_element_type=jnp.float32)

        def pass2(c, carry):
            cols = pl.ds(pl.multiple_of(c * chunk, chunk), chunk)

            @pl.when(c < first)
            def _():
                w_scr[:, cols] = jnp.zeros((rows, chunk), jnp.bfloat16)

            @pl.when(c >= first)
            def _():
                w_scr[:, cols] = (expo_scr[c] * inv).astype(jnp.bfloat16)

            return carry

        lax.fori_loop(0, nchunks, pass2, 0)
        vw = v_ref[pl.ds(pl.multiple_of(q0, chunk), win), :]
        out = acc_scr[...] + jnp.dot(w_scr[...], vw, preferred_element_type=jnp.float32)
        out16 = out.astype(jnp.bfloat16)
        for g in range(group):
            o_ref[:, g * HEAD:(g + 1) * HEAD] = out16[g * tq:(g + 1) * tq]
            ss_ref[0, g] = ssum[g * tq:(g + 1) * tq]

    off = jnp.reshape(offset, (1,)).astype(jnp.int32)
    return pl.pallas_call(
        kernel,
        out_shape=(
            jax.ShapeDtypeStruct((tok_rows, local_kv * group * HEAD), jnp.bfloat16),
            jax.ShapeDtypeStruct((local_kv, group, tok_rows, 1), jnp.float32),
        ),
        grid_spec=pltpu.PrefetchScalarGridSpec(
            num_scalar_prefetch=1,
            grid=(local_kv, n_qt),
            in_specs=[
                pl.BlockSpec((tq, group * HEAD), lambda k, i, o: (i, k)),
                pl.BlockSpec((tq, HEAD), lambda k, i, o: (i, 0)),
                pl.BlockSpec((tq, HEAD), lambda k, i, o: (i, 0)),
                pl.BlockSpec((pad_rows, HEAD), lambda k, i, o: (0, k)),
                pl.BlockSpec((pad_rows, HEAD), lambda k, i, o: (0, local_kv + k)),
            ] + [pl.BlockSpec(memory_space=pl.ANY) for _ in tuple(pieces) + tuple(extra)],
            out_specs=[
                pl.BlockSpec((tq, group * HEAD), lambda k, i, o: (i, k)),
                pl.BlockSpec((1, group, tq, 1), lambda k, i, o: (k, 0, i, 0)),
            ],
            scratch_shapes=[
                pltpu.VMEM((nchunks, rows, chunk), jnp.float32),
                pltpu.VMEM((rows, HEAD), jnp.float32),
                pltpu.VMEM((rows, 128), jnp.float32),
                pltpu.VMEM((span, HEAD), jnp.bfloat16),
                pltpu.VMEM((span, HEAD), jnp.bfloat16),
                pltpu.VMEM((rows, win), jnp.bfloat16),
                pltpu.SemaphoreType.DMA((2, len(orders[0]))),
            ],
        ),
        compiler_params=pltpu.CompilerParams(dimension_semantics=("arbitrary", "arbitrary")),
    )(off, query, cosine, sine, sink_pad, sink_pad, *pieces, *extra)


def on_device(hidden_in, pre_gain, w_query, w_key, w_value, w_out, post_gain):
    tok_rows = hidden_in.shape[0]
    local_q = w_query.shape[1] // HEAD
    local_kv = w_key.shape[1] // HEAD
    group = local_q // local_kv
    tp_n = lax.axis_size("tp")
    tp_i = lax.axis_index("tp")
    cols_dev = post_gain.shape[0]

    w_recv = []
    for k in range(tp_n):
        part = lax.dynamic_slice_in_dim(w_out, ((tp_i + k) % tp_n) * cols_dev, cols_dev, 1)
        w_recv.append(part if k == 0 else cyclic(part, "tp", k))

    offset = lax.axis_index("ctx") * tok_rows
    inputs = hidden_in.astype(jnp.float32)
    normed = (
        inputs * lax.rsqrt(jnp.mean(inputs * inputs, axis=-1, keepdims=True) + 1e-06) * pre_gain
    ).astype(jnp.bfloat16)
    positions = offset + jnp.arange(tok_rows, dtype=jnp.int32)
    cosine_table, sine_table = rope_tables(positions)
    query = jnp.dot(normed, w_query, preferred_element_type=jnp.float32)
    keys = jnp.dot(normed, w_key, preferred_element_type=jnp.float32).reshape(tok_rows, -1, HEAD)
    keys = rotate(keys, cosine_table, sine_table).astype(jnp.bfloat16).reshape(tok_rows, -1)
    values = jnp.dot(normed, w_value, preferred_element_type=jnp.float32).astype(jnp.bfloat16)
    kv = jnp.concatenate([keys, values], axis=1)

    sink_kv = from_first(kv[:SINKS], "ctx")
    sink_pad = jnp.zeros((HEAD, sink_kv.shape[1]), sink_kv.dtype).at[:SINKS].set(sink_kv)
    reach = WINDOW // tok_rows
    pieces = [shifted(kv, "ctx", distance) for distance in range(reach, 0, -1)] + [kv]
    orders = (tuple(range(len(pieces))),)
    attended, sink_parts = window_attention(
        query, cosine_table[:, 0, :], sine_table[:, 0, :], pieces, orders, sink_pad, offset, local_kv, group,
        extra=tuple(w_recv[1:]),
    )
    sink_sums = jnp.sum(sink_parts[..., 0], axis=(0, 1))
    projected = jnp.dot(attended, w_recv[0], preferred_element_type=jnp.float32)
    for k in range(1, tp_n):
        projected = projected + jnp.dot(
            cyclic(attended, "tp", k), w_recv[k], preferred_element_type=jnp.float32
        )
    squares = jnp.sum(projected * projected, axis=-1)
    total_squares, total_sinks = lax.psum((squares, sink_sums), "tp")
    post = projected * lax.rsqrt(total_squares / D + 1e-06)[:, None] * post_gain
    own_cols = lax.dynamic_slice_in_dim(hidden_in, tp_i * cols_dev, cols_dev, 1).astype(jnp.float32)
    layer_out = (own_cols + post).astype(jnp.bfloat16)
    sink_share = jnp.log(total_sinks / QHEADS)
    return (layer_out, sink_share)


def solution(mesh):
    return jax.shard_map(
        on_device,
        mesh=mesh,
        in_specs=(
            P("ctx", None),
            P(),
            P(None, "tp"),
            P(None, "tp"),
            P(None, "tp"),
            P("tp", None),
            P("tp"),
        ),
        out_specs=(P("ctx", "tp"), P("ctx")),
        check_vma=False,
    )
```

```python
import math

import jax
import jax.numpy as jnp
from jax import lax
from jax.experimental import pallas as pl
from jax.experimental.pallas import tpu as pltpu
from jax.sharding import PartitionSpec as P


D = 4608
QHEADS = 16
HEAD = 128
WINDOW = 4096
SINKS = 4
EXP_SCALE = 50.0 / math.log(2.0)


def shifted(x, axis, by):
    devices = lax.axis_size(axis)
    pairs = [(i, i + by) for i in range(devices) if 0 <= i + by < devices]
    return lax.ppermute(x, axis, pairs)


def cyclic(x, axis, by):
    devices = lax.axis_size(axis)
    return lax.ppermute(x, axis, [(i, (i + by) % devices) for i in range(devices)])


def from_first(x, axis):
    devices = lax.axis_size(axis)
    index = lax.axis_index(axis)
    step = devices // 2
    while step >= 1:
        pairs = [(i, i + step) for i in range(0, devices, 2 * step)]
        got = lax.ppermute(x, axis, pairs)
        x = jnp.where(index % (2 * step) == step, got, x)
        step //= 2
    return x


def rope_tables(positions):
    index = jnp.arange(0, HEAD, 2).astype(jnp.float32)
    inverse = jnp.exp(-jnp.log(jnp.float32(10000.0)) * index / HEAD)
    angles = positions.astype(jnp.float32)[:, None] * inverse[None, :]
    angles = jnp.concatenate([angles, angles], axis=1)
    return (jnp.cos(angles)[:, None, :], jnp.sin(angles)[:, None, :])


def rotate(values, cosine_table, sine_table):
    half = values.shape[-1] // 2
    turned = jnp.concatenate([-values[..., half:], values[..., :half]], axis=-1)
    return values * cosine_table + turned * sine_table


def window_attention(query, cosine, sine, pieces, orders, sink_pad, offset, local_kv, group, extra=(), tq=256, chunk=256):
    tok_rows = query.shape[0]
    n_qt = tok_rows // tq
    piece_rows = pieces[0].shape[0]
    n_pieces = len(pieces)
    span = piece_rows * len(orders[0])
    rows = group * tq
    win = WINDOW + tq
    nchunks = win // chunk
    pad_rows = sink_pad.shape[0]

    def kernel(off_ref, q_ref, cos_ref, sin_ref, sk_ref, sv_ref, *rest):
        piece_refs = rest[:n_pieces]
        o_ref, ss_ref, expo_scr, acc_scr, rs_scr, k_ref, v_ref, w_scr, sems = rest[n_pieces + len(extra):]
        k = pl.program_id(0)
        i = pl.program_id(1)

        parity = (off_ref[0] // piece_rows) % len(orders)

        def fetch(order):
            copies = []
            for p, src in enumerate(order):
                rows_p = pl.ds(p * piece_rows, piece_rows)
                copies.append(pltpu.make_async_copy(
                    piece_refs[src].at[:, pl.ds(k * HEAD, HEAD)], k_ref.at[rows_p, :], sems.at[0, p]))
                copies.append(pltpu.make_async_copy(
                    piece_refs[src].at[:, pl.ds((local_kv + k) * HEAD, HEAD)], v_ref.at[rows_p, :], sems.at[1, p]))
            for cp in copies:
                cp.start()
            for cp in copies:
                cp.wait()

        for which, order in enumerate(orders):
            pl.when((i == 0) & (parity == which))(lambda order=order: fetch(order))

        q0 = i * tq
        base = off_ref[0] - WINDOW + q0
        half = lax.broadcasted_iota(jnp.int32, (1, HEAD), 1) < HEAD // 2
        sign = jnp.where(half, -1.0, 1.0).astype(jnp.float32)
        cos_t = cos_ref[...]
        sin_t = sin_ref[...]
        heads = []
        for g in range(group):
            x = q_ref[:, g * HEAD:(g + 1) * HEAD]
            turned = pltpu.roll(x, HEAD // 2, 1) * sign
            heads.append((x * cos_t + turned * sin_t).astype(jnp.bfloat16))
        q = jnp.concatenate(heads, axis=0)
        qi = lax.broadcasted_iota(jnp.int32, (rows, 1), 0) % tq
        lo = jnp.maximum(qi + 1, SINKS - base)
        hi = qi + WINDOW
        first = jnp.maximum(SINKS - base, 0) // chunk
        rs_scr[...] = jnp.zeros((rows, 128), jnp.float32)

        def keep(c, e):
            expo_scr[c] = e
            part = e[:, 0:128]
            for h in range(1, chunk // 128):
                part = part + e[:, h * 128:(h + 1) * 128]
            rs_scr[...] += part

        def squash(c):
            start = pl.multiple_of(q0 + c * chunk, chunk)
            kc = k_ref[pl.ds(start, chunk), :]
            s = lax.dot_general(q, kc, (((1,), (1,)), ((), ())), preferred_element_type=jnp.float32)
            return jnp.tanh(s * (1.0 / 600.0))

        def pass1(c, carry):
            edge = (c * chunk < tq) | ((c + 1) * chunk > WINDOW + 1) | (base + c * chunk < SINKS)

            @pl.when(edge)
            def _():
                u = squash(c)
                col = c * chunk + lax.broadcasted_iota(jnp.int32, (1, chunk), 1)
                live = (col >= lo) & (col <= hi)
                keep(c, jnp.where(live, jnp.exp2(u * EXP_SCALE), 0.0))

            @pl.when(jnp.logical_not(edge))
            def _():
                keep(c, jnp.exp2(squash(c) * EXP_SCALE))

            return carry

        lax.fori_loop(first, nchunks, pass1, 0)
        rowsum = jnp.sum(rs_scr[...], axis=1, keepdims=True)
        ssc = lax.dot_general(q, sk_ref[...], (((1,), (1,)), ((), ())), preferred_element_type=jnp.float32)
        su = jnp.tanh(ssc * (1.0 / 600.0))
        scol = lax.broadcasted_iota(jnp.int32, (1, pad_rows), 1)
        qpos = off_ref[0] + q0 + qi
        slive = (scol < SINKS) & (qpos >= scol)
        se = jnp.where(slive, jnp.exp2(su * EXP_SCALE), 0.0)
        ssum = jnp.sum(se, axis=1, keepdims=True)
        total = rowsum + ssum
        inv = 1.0 / total
        sw = (se * inv).astype(jnp.bfloat16)
        acc_scr[...] = jnp.dot(sw, sv_ref[...], preferred_element_type=jnp.float32)

        def pass2(c, carry):
            cols = pl.ds(pl.multiple_of(c * chunk, chunk), chunk)

            @pl.when(c < first)
            def _():
                w_scr[:, cols] = jnp.zeros((rows, chunk), jnp.bfloat16)

            @pl.when(c >= first)
            def _():
                w_scr[:, cols] = (expo_scr[c] * inv).astype(jnp.bfloat16)

            return carry

        lax.fori_loop(0, nchunks, pass2, 0)
        vw = v_ref[pl.ds(pl.multiple_of(q0, chunk), win), :]
        out = acc_scr[...] + jnp.dot(w_scr[...], vw, preferred_element_type=jnp.float32)
        out16 = out.astype(jnp.bfloat16)
        for g in range(group):
            o_ref[:, g * HEAD:(g + 1) * HEAD] = out16[g * tq:(g + 1) * tq]
            ss_ref[0, g] = ssum[g * tq:(g + 1) * tq]

    off = jnp.reshape(offset, (1,)).astype(jnp.int32)
    return pl.pallas_call(
        kernel,
        out_shape=(
            jax.ShapeDtypeStruct((tok_rows, local_kv * group * HEAD), jnp.bfloat16),
            jax.ShapeDtypeStruct((local_kv, group, tok_rows, 1), jnp.float32),
        ),
        grid_spec=pltpu.PrefetchScalarGridSpec(
            num_scalar_prefetch=1,
            grid=(local_kv, n_qt),
            in_specs=[
                pl.BlockSpec((tq, group * HEAD), lambda k, i, o: (i, k)),
                pl.BlockSpec((tq, HEAD), lambda k, i, o: (i, 0)),
                pl.BlockSpec((tq, HEAD), lambda k, i, o: (i, 0)),
                pl.BlockSpec((pad_rows, HEAD), lambda k, i, o: (0, k)),
                pl.BlockSpec((pad_rows, HEAD), lambda k, i, o: (0, local_kv + k)),
            ] + [pl.BlockSpec(memory_space=pl.ANY) for _ in tuple(pieces) + tuple(extra)],
            out_specs=[
                pl.BlockSpec((tq, group * HEAD), lambda k, i, o: (i, k)),
                pl.BlockSpec((1, group, tq, 1), lambda k, i, o: (k, 0, i, 0)),
            ],
            scratch_shapes=[
                pltpu.VMEM((nchunks, rows, chunk), jnp.float32),
                pltpu.VMEM((rows, HEAD), jnp.float32),
                pltpu.VMEM((rows, 128), jnp.float32),
                pltpu.VMEM((span, HEAD), jnp.bfloat16),
                pltpu.VMEM((span, HEAD), jnp.bfloat16),
                pltpu.VMEM((rows, win), jnp.bfloat16),
                pltpu.SemaphoreType.DMA((2, len(orders[0]))),
            ],
        ),
        compiler_params=pltpu.CompilerParams(dimension_semantics=("arbitrary", "arbitrary")),
    )(off, query, cosine, sine, sink_pad, sink_pad, *pieces, *extra)


def on_device(hidden_in, pre_gain, w_query, w_key, w_value, w_out, post_gain):
    tok_rows = hidden_in.shape[0]
    local_q = w_query.shape[1] // HEAD
    local_kv = w_key.shape[1] // HEAD
    group = local_q // local_kv
    tp_n = lax.axis_size("tp")
    tp_i = lax.axis_index("tp")
    cols_dev = post_gain.shape[0]

    w_recv = []
    for k in range(tp_n):
        part = lax.dynamic_slice_in_dim(w_out, ((tp_i + k) % tp_n) * cols_dev, cols_dev, 1)
        w_recv.append(part if k == 0 else cyclic(part, "tp", k))

    offset = lax.axis_index("ctx") * tok_rows
    inputs = hidden_in.astype(jnp.float32)
    normed = (
        inputs * lax.rsqrt(jnp.mean(inputs * inputs, axis=-1, keepdims=True) + 1e-06) * pre_gain
    ).astype(jnp.bfloat16)
    positions = offset + jnp.arange(tok_rows, dtype=jnp.int32)
    cosine_table, sine_table = rope_tables(positions)
    query = jnp.dot(normed, w_query, preferred_element_type=jnp.float32)
    keys = jnp.dot(normed, w_key, preferred_element_type=jnp.float32).reshape(tok_rows, -1, HEAD)
    keys = rotate(keys, cosine_table, sine_table).astype(jnp.bfloat16).reshape(tok_rows, -1)
    values = jnp.dot(normed, w_value, preferred_element_type=jnp.float32).astype(jnp.bfloat16)
    kv = jnp.concatenate([keys, values], axis=1)

    sink_rows = from_first(hidden_in[:SINKS], "ctx").astype(jnp.float32)
    sink_normed = (
        sink_rows * lax.rsqrt(jnp.mean(sink_rows * sink_rows, axis=-1, keepdims=True) + 1e-06) * pre_gain
    ).astype(jnp.bfloat16)
    sink_cos, sink_sin = rope_tables(jnp.arange(SINKS, dtype=jnp.int32))
    sink_keys = jnp.dot(sink_normed, w_key, preferred_element_type=jnp.float32).reshape(SINKS, -1, HEAD)
    sink_keys = rotate(sink_keys, sink_cos, sink_sin).astype(jnp.bfloat16).reshape(SINKS, -1)
    sink_values = jnp.dot(sink_normed, w_value, preferred_element_type=jnp.float32).astype(jnp.bfloat16)
    sink_kv = jnp.concatenate([sink_keys, sink_values], axis=1)
    sink_pad = jnp.zeros((HEAD, sink_kv.shape[1]), sink_kv.dtype).at[:SINKS].set(sink_kv)
    reach = WINDOW // tok_rows
    ctx_n = lax.axis_size("ctx")
    fetched = [shifted(kv, "ctx", distance) for distance in range(reach, 0, -2)]
    swap_pairs = [(i, i ^ 1) for i in range(ctx_n)]
    swapped = [lax.ppermute(x, "ctx", swap_pairs) for x in fetched + [kv]]
    pieces = fetched + swapped + [kv]
    own = len(pieces) - 1
    half = len(fetched)
    even_order, odd_order = [], []
    for j in range(half):
        even_order += [j, half + j]
        odd_order += [j, half + j + 1]
    orders = (tuple(even_order + [own]), tuple(odd_order + [own]))
    attended, sink_parts = window_attention(
        query, cosine_table[:, 0, :], sine_table[:, 0, :], pieces, orders, sink_pad, offset, local_kv, group,
        extra=tuple(w_recv[1:]),
    )
    sink_sums = jnp.sum(sink_parts[..., 0], axis=(0, 1))
    projected = jnp.dot(attended, w_recv[0], preferred_element_type=jnp.float32)
    for k in range(1, tp_n):
        projected = projected + jnp.dot(
            cyclic(attended, "tp", k), w_recv[k], preferred_element_type=jnp.float32
        )
    squares = jnp.sum(projected * projected, axis=-1)
    total_squares, total_sinks = lax.psum((squares, sink_sums), "tp")
    post = projected * lax.rsqrt(total_squares / D + 1e-06)[:, None] * post_gain
    own_cols = lax.dynamic_slice_in_dim(hidden_in, tp_i * cols_dev, cols_dev, 1).astype(jnp.float32)
    layer_out = (own_cols + post).astype(jnp.bfloat16)
    sink_share = jnp.log(total_sinks / QHEADS)
    return (layer_out, sink_share)


def solution(mesh):
    return jax.shard_map(
        on_device,
        mesh=mesh,
        in_specs=(
            P("ctx", None),
            P(),
            P(None, "tp"),
            P(None, "tp"),
            P(None, "tp"),
            P("tp", None),
            P("tp"),
        ),
        out_specs=(P("ctx", "tp"), P("ctx")),
        check_vma=False,
    )
```

```python
import math

import jax
import jax.numpy as jnp
from jax import lax
from jax.experimental import pallas as pl
from jax.experimental.pallas import tpu as pltpu
from jax.sharding import PartitionSpec as P


D = 4608
QHEADS = 16
HEAD = 128
WINDOW = 4096
SINKS = 4
EXP_SCALE = 50.0 / math.log(2.0)


def shifted(x, axis, by):
    devices = lax.axis_size(axis)
    pairs = [(i, i + by) for i in range(devices) if 0 <= i + by < devices]
    return lax.ppermute(x, axis, pairs)


def cyclic(x, axis, by):
    devices = lax.axis_size(axis)
    return lax.ppermute(x, axis, [(i, (i + by) % devices) for i in range(devices)])


def from_first(x, axis):
    devices = lax.axis_size(axis)
    index = lax.axis_index(axis)
    span = devices
    while span > 1:
        fan = 4 if span % 4 == 0 else 2
        stride = span // fan
        sent = x
        for k in range(1, fan):
            pairs = [(i, i + k * stride) for i in range(0, devices, span)]
            got = lax.ppermute(x, axis, pairs)
            sent = jnp.where(index % span == k * stride, got, sent)
        x = sent
        span = stride
    return x


def rope_tables(positions):
    index = jnp.arange(0, HEAD, 2).astype(jnp.float32)
    inverse = jnp.exp(-jnp.log(jnp.float32(10000.0)) * index / HEAD)
    angles = positions.astype(jnp.float32)[:, None] * inverse[None, :]
    angles = jnp.concatenate([angles, angles], axis=1)
    return (jnp.cos(angles)[:, None, :], jnp.sin(angles)[:, None, :])


def rotate(values, cosine_table, sine_table):
    half = values.shape[-1] // 2
    turned = jnp.concatenate([-values[..., half:], values[..., :half]], axis=-1)
    return values * cosine_table + turned * sine_table


def window_attention(query, cosine, sine, pieces, orders, sink_pad, offset, local_kv, group, extra=(), tq=256, chunk=256):
    tok_rows = query.shape[0]
    n_qt = tok_rows // tq
    piece_rows = pieces[0].shape[0]
    n_pieces = len(pieces)
    span = piece_rows * len(orders[0])
    rows = group * tq
    win = WINDOW + tq
    nchunks = win // chunk
    pad_rows = sink_pad.shape[0]

    def kernel(off_ref, q_ref, cos_ref, sin_ref, sk_ref, sv_ref, *rest):
        piece_refs = rest[:n_pieces]
        o_ref, ss_ref, expo_scr, acc_scr, rs_scr, k_ref, v_ref, w_scr, sems = rest[n_pieces + len(extra):]
        k = pl.program_id(0)
        i = pl.program_id(1)

        parity = (off_ref[0] // piece_rows) % len(orders)

        def fetch(order):
            copies = []
            for p, src in enumerate(order):
                rows_p = pl.ds(p * piece_rows, piece_rows)
                copies.append(pltpu.make_async_copy(
                    piece_refs[src].at[:, pl.ds(k * HEAD, HEAD)], k_ref.at[rows_p, :], sems.at[0, p]))
                copies.append(pltpu.make_async_copy(
                    piece_refs[src].at[:, pl.ds((local_kv + k) * HEAD, HEAD)], v_ref.at[rows_p, :], sems.at[1, p]))
            for cp in copies:
                cp.start()
            for cp in copies:
                cp.wait()

        for which, order in enumerate(orders):
            pl.when((i == 0) & (parity == which))(lambda order=order: fetch(order))

        q0 = i * tq
        base = off_ref[0] - WINDOW + q0
        half = lax.broadcasted_iota(jnp.int32, (1, HEAD), 1) < HEAD // 2
        sign = jnp.where(half, -1.0, 1.0).astype(jnp.float32)
        cos_t = cos_ref[...]
        sin_t = sin_ref[...]
        heads = []
        for g in range(group):
            x = q_ref[:, g * HEAD:(g + 1) * HEAD]
            turned = pltpu.roll(x, HEAD // 2, 1) * sign
            heads.append((x * cos_t + turned * sin_t).astype(jnp.bfloat16))
        q = jnp.concatenate(heads, axis=0)
        qi = lax.broadcasted_iota(jnp.int32, (rows, 1), 0) % tq
        lo = jnp.maximum(qi + 1, SINKS - base)
        hi = qi + WINDOW
        first = jnp.maximum(SINKS - base, 0) // chunk
        rs_scr[...] = jnp.zeros((rows, 128), jnp.float32)

        def keep(c, e):
            expo_scr[c] = e
            part = e[:, 0:128]
            for h in range(1, chunk // 128):
                part = part + e[:, h * 128:(h + 1) * 128]
            rs_scr[...] += part

        def squash(c):
            start = pl.multiple_of(q0 + c * chunk, chunk)
            kc = k_ref[pl.ds(start, chunk), :]
            s = lax.dot_general(q, kc, (((1,), (1,)), ((), ())), preferred_element_type=jnp.float32)
            return jnp.tanh(s * (1.0 / 600.0))

        def pass1(c, carry):
            edge = (c * chunk < tq) | ((c + 1) * chunk > WINDOW + 1) | (base + c * chunk < SINKS)

            @pl.when(edge)
            def _():
                u = squash(c)
                col = c * chunk + lax.broadcasted_iota(jnp.int32, (1, chunk), 1)
                live = (col >= lo) & (col <= hi)
                keep(c, jnp.where(live, jnp.exp2(u * EXP_SCALE), 0.0))

            @pl.when(jnp.logical_not(edge))
            def _():
                keep(c, jnp.exp2(squash(c) * EXP_SCALE))

            return carry

        lax.fori_loop(first, nchunks, pass1, 0)
        rowsum = jnp.sum(rs_scr[...], axis=1, keepdims=True)
        ssc = lax.dot_general(q, sk_ref[...], (((1,), (1,)), ((), ())), preferred_element_type=jnp.float32)
        su = jnp.tanh(ssc * (1.0 / 600.0))
        scol = lax.broadcasted_iota(jnp.int32, (1, pad_rows), 1)
        qpos = off_ref[0] + q0 + qi
        slive = (scol < SINKS) & (qpos >= scol)
        se = jnp.where(slive, jnp.exp2(su * EXP_SCALE), 0.0)
        ssum = jnp.sum(se, axis=1, keepdims=True)
        total = rowsum + ssum
        inv = 1.0 / total
        sw = (se * inv).astype(jnp.bfloat16)
        acc_scr[...] = jnp.dot(sw, sv_ref[...], preferred_element_type=jnp.float32)

        def pass2(c, carry):
            cols = pl.ds(pl.multiple_of(c * chunk, chunk), chunk)

            @pl.when(c < first)
            def _():
                w_scr[:, cols] = jnp.zeros((rows, chunk), jnp.bfloat16)

            @pl.when(c >= first)
            def _():
                w_scr[:, cols] = (expo_scr[c] * inv).astype(jnp.bfloat16)

            return carry

        lax.fori_loop(0, nchunks, pass2, 0)
        vw = v_ref[pl.ds(pl.multiple_of(q0, chunk), win), :]
        out = acc_scr[...] + jnp.dot(w_scr[...], vw, preferred_element_type=jnp.float32)
        out16 = out.astype(jnp.bfloat16)
        for g in range(group):
            o_ref[:, g * HEAD:(g + 1) * HEAD] = out16[g * tq:(g + 1) * tq]
            ss_ref[0, g] = ssum[g * tq:(g + 1) * tq]

    off = jnp.reshape(offset, (1,)).astype(jnp.int32)
    return pl.pallas_call(
        kernel,
        out_shape=(
            jax.ShapeDtypeStruct((tok_rows, local_kv * group * HEAD), jnp.bfloat16),
            jax.ShapeDtypeStruct((local_kv, group, tok_rows, 1), jnp.float32),
        ),
        grid_spec=pltpu.PrefetchScalarGridSpec(
            num_scalar_prefetch=1,
            grid=(local_kv, n_qt),
            in_specs=[
                pl.BlockSpec((tq, group * HEAD), lambda k, i, o: (i, k)),
                pl.BlockSpec((tq, HEAD), lambda k, i, o: (i, 0)),
                pl.BlockSpec((tq, HEAD), lambda k, i, o: (i, 0)),
                pl.BlockSpec((pad_rows, HEAD), lambda k, i, o: (0, k)),
                pl.BlockSpec((pad_rows, HEAD), lambda k, i, o: (0, local_kv + k)),
            ] + [pl.BlockSpec(memory_space=pl.ANY) for _ in tuple(pieces) + tuple(extra)],
            out_specs=[
                pl.BlockSpec((tq, group * HEAD), lambda k, i, o: (i, k)),
                pl.BlockSpec((1, group, tq, 1), lambda k, i, o: (k, 0, i, 0)),
            ],
            scratch_shapes=[
                pltpu.VMEM((nchunks, rows, chunk), jnp.float32),
                pltpu.VMEM((rows, HEAD), jnp.float32),
                pltpu.VMEM((rows, 128), jnp.float32),
                pltpu.VMEM((span, HEAD), jnp.bfloat16),
                pltpu.VMEM((span, HEAD), jnp.bfloat16),
                pltpu.VMEM((rows, win), jnp.bfloat16),
                pltpu.SemaphoreType.DMA((2, len(orders[0]))),
            ],
        ),
        compiler_params=pltpu.CompilerParams(dimension_semantics=("arbitrary", "arbitrary")),
    )(off, query, cosine, sine, sink_pad, sink_pad, *pieces, *extra)


def on_device(hidden_in, pre_gain, w_query, w_key, w_value, w_out, post_gain):
    tok_rows = hidden_in.shape[0]
    local_q = w_query.shape[1] // HEAD
    local_kv = w_key.shape[1] // HEAD
    group = local_q // local_kv
    tp_n = lax.axis_size("tp")
    tp_i = lax.axis_index("tp")
    cols_dev = post_gain.shape[0]

    w_recv = []
    for k in range(tp_n):
        part = lax.dynamic_slice_in_dim(w_out, ((tp_i + k) % tp_n) * cols_dev, cols_dev, 1)
        w_recv.append(part if k == 0 else cyclic(part, "tp", k))

    offset = lax.axis_index("ctx") * tok_rows
    inputs = hidden_in.astype(jnp.float32)
    normed = (
        inputs * lax.rsqrt(jnp.mean(inputs * inputs, axis=-1, keepdims=True) + 1e-06) * pre_gain
    ).astype(jnp.bfloat16)
    positions = offset + jnp.arange(tok_rows, dtype=jnp.int32)
    cosine_table, sine_table = rope_tables(positions)
    query = jnp.dot(normed, w_query, preferred_element_type=jnp.float32)
    keys = jnp.dot(normed, w_key, preferred_element_type=jnp.float32).reshape(tok_rows, -1, HEAD)
    keys = rotate(keys, cosine_table, sine_table).astype(jnp.bfloat16).reshape(tok_rows, -1)
    values = jnp.dot(normed, w_value, preferred_element_type=jnp.float32).astype(jnp.bfloat16)
    kv = jnp.concatenate([keys, values], axis=1)

    sink_rows = from_first(hidden_in[:SINKS], "ctx").astype(jnp.float32)
    sink_normed = (
        sink_rows * lax.rsqrt(jnp.mean(sink_rows * sink_rows, axis=-1, keepdims=True) + 1e-06) * pre_gain
    ).astype(jnp.bfloat16)
    sink_cos, sink_sin = rope_tables(jnp.arange(SINKS, dtype=jnp.int32))
    sink_keys = jnp.dot(sink_normed, w_key, preferred_element_type=jnp.float32).reshape(SINKS, -1, HEAD)
    sink_keys = rotate(sink_keys, sink_cos, sink_sin).astype(jnp.bfloat16).reshape(SINKS, -1)
    sink_values = jnp.dot(sink_normed, w_value, preferred_element_type=jnp.float32).astype(jnp.bfloat16)
    sink_kv = jnp.concatenate([sink_keys, sink_values], axis=1)
    sink_pad = jnp.zeros((HEAD, sink_kv.shape[1]), sink_kv.dtype).at[:SINKS].set(sink_kv)
    reach = WINDOW // tok_rows
    ctx_n = lax.axis_size("ctx")
    fetched = [shifted(kv, "ctx", distance) for distance in range(reach, 0, -2)]
    swap_pairs = [(i, i ^ 1) for i in range(ctx_n)]
    swapped = [lax.ppermute(x, "ctx", swap_pairs) for x in fetched + [kv]]
    pieces = fetched + swapped + [kv]
    own = len(pieces) - 1
    half = len(fetched)
    even_order, odd_order = [], []
    for j in range(half):
        even_order += [j, half + j]
        odd_order += [j, half + j + 1]
    orders = (tuple(even_order + [own]), tuple(odd_order + [own]))
    attended, sink_parts = window_attention(
        query, cosine_table[:, 0, :], sine_table[:, 0, :], pieces, orders, sink_pad, offset, local_kv, group,
        extra=tuple(w_recv[1:]),
    )
    sink_sums = jnp.sum(sink_parts[..., 0], axis=(0, 1))
    projected = jnp.dot(attended, w_recv[0], preferred_element_type=jnp.float32)
    for k in range(1, tp_n):
        projected = projected + jnp.dot(
            cyclic(attended, "tp", k), w_recv[k], preferred_element_type=jnp.float32
        )
    squares = jnp.sum(projected * projected, axis=-1)
    total_squares, total_sinks = lax.psum((squares, sink_sums), "tp")
    post = projected * lax.rsqrt(total_squares / D + 1e-06)[:, None] * post_gain
    own_cols = lax.dynamic_slice_in_dim(hidden_in, tp_i * cols_dev, cols_dev, 1).astype(jnp.float32)
    layer_out = (own_cols + post).astype(jnp.bfloat16)
    sink_share = jnp.log(total_sinks / QHEADS)
    return (layer_out, sink_share)


def solution(mesh):
    return jax.shard_map(
        on_device,
        mesh=mesh,
        in_specs=(
            P("ctx", None),
            P(),
            P(None, "tp"),
            P(None, "tp"),
            P(None, "tp"),
            P("tp", None),
            P("tp"),
        ),
        out_specs=(P("ctx", "tp"), P("ctx")),
        check_vma=False,
    )
```
